32 devices in a mesh: gz: 8 (over z, x), gy: 4 (over y, core).
Axes of the slice: x: 2, y: 2, z: 4, core: 2. Of those that a mesh axis runs over, the one named last changes fastest.
Arguments:
- velocity: float32 [3, 16, 8, 128], P(None, 'gz', 'gy'), may hold values from -6 to 6
- slip: float32 [3, 16384], P(None, ('gz', 'gy')), may hold values from -6 to 6
- rate: float32 [16384], P(('gz', 'gy')), may hold values from 0.5 to 4
- owner: int32 [16384, 1], P(('gz', 'gy')), may hold values from 0 to 7; in each aligned block of 512 rows (0 to 511, 512 to 1023, ...) at most 128 rows name the same one
- cell: int32 [16384], P(('gz', 'gy')), may hold values from 0 to 511
- count: int32 [32], P(('gz', 'gy')), may hold values from 256 to 512
- w_in: bfloat16 [12, 1024], replicated, may hold values from -1.75 to 1.75
- b_in: float32 [1024], replicated, may hold values from -3 to 3
- w_mid: bfloat16 [1024, 1024], replicated, may hold values from -0.1875 to 0.1875
- b_mid: float32 [1024], replicated, may hold values from -3 to 3
- w_out: bfloat16 [1024, 6], replicated, may hold values from -0.1875 to 0.1875
- tau_bar: bfloat16 [6, 16, 8, 128], P(None, 'gz', 'gy'), may hold values from -1.5 to 1.5
Outputs:
- stress: float32 [6, 16, 8, 128], P(None, 'gz', 'gy')
- velocity_bar: float32 [3, 16, 8, 128], P(None, 'gz', 'gy')
- slip_bar: float32 [3, 16384], P(None, ('gz', 'gy'))
- rate_bar: float32 [16384], P(('gz', 'gy'))
- grad_w_in: float32 [12, 1024], replicated
- grad_b_in: float32 [1024], replicated
- grad_w_mid: float32 [1024, 1024], replicated
- grad_b_mid: float32 [1024], replicated
- grad_w_out: float32 [1024, 6], replicated
The draws below stay inside these ranges and needn't reach their ends.
Inputs may be any that keep to these rules, and one draw needn't show every extreme that they name: Each particle's cell lies in the slab owner names, in the y-range of the particle's own device index along gy. Among the 512 slots of one device, at most 128 name the same slab, and that many do for some slab. The cell is flattened in the order z, y, x of the owner's block. The first count slots of a device are live, the others empty.
All inputs are finite; a program needn't handle non-finite values.
Results may differ from the reference program's by a relative error of at most 0.007.
Values sent between devices are 32-bit elements; how exact they have to be, the bound alone decides.
No kernel may reach another device: no remote copies, remote signals or barrier semaphores. Data moves between devices by JAX's collectives and lax.ppermute only.
A program may use at most 64 MiB of HBM per device.

```python
import math
import jax
import jax.numpy as jnp
import numpy as np
from jax import lax

CZ = 2
CY = 2
NX = 128
H = 1024
F_IN = 12
N_OUT = 6
P_DEV = 512
CAP = 128
CELLS_DEV = 512
NZ = 16
NY = 8
PARTS_SIZE = 16384
N_GZ = 8
N_GY = 4


def place_ends(values, rng, low, largest):
    extent = values.shape
    spot = [jax.random.randint(jax.random.fold_in(rng, axis), (), 0, extent[axis]) for axis in range(len(extent))]
    values = values.at[tuple(spot)].set(low)
    longest = extent.index(max(extent))
    spot[longest] = (spot[longest] + 1) % extent[longest]
    return values.at[tuple(spot)].set(largest)


def block_levels(rng, shape, split, smallest, high):
    def one(position, parts):
        steps = jax.random.uniform(jax.random.fold_in(jax.random.fold_in(rng, 6), position), (parts,), jnp.float32, smallest / len(split), high / len(split))
        return jnp.repeat(jnp.exp(steps), shape[position] // parts).reshape((-1,) + (1,) * (len(shape) - position - 1))

    gain = one(*split[0])
    for cut in split[1:]:
        gain = gain * one(*cut)
    return gain


def cumulative_ranks(amount, slope):
    loads = [(1 << 20) // math.isqrt(standing ** slope) + 1 for standing in range(1, amount + 1)]
    width = 1 + sum(loads) // (1 << 30)
    return np.cumsum(np.array([max(1, weight // width) for weight in loads]))


def skewed_ids(key, extent, amount, lean):
    grid = cumulative_ranks(amount, lean)
    ticket = jax.random.randint(jax.random.fold_in(key, 1), extent, 0, int(grid[amount - 1]))
    standing = jnp.searchsorted(jnp.asarray(grid, jnp.int32), ticket, side="right")
    return jax.random.permutation(jax.random.fold_in(key, 2), amount)[standing].astype(jnp.int32)


def shared_out(stream_key, own, number, rows, number_of, top, limit, slope):
    sequence = jax.random.permutation(stream_key, number_of)
    crowded, usual = shares(number_of, rows * top, limit, slope, True), shares(number_of, rows * top, limit, slope, False)
    places = jnp.arange(number_of)

    def named(sizes, offset_by):
        used = int((sizes > 0).sum())
        fixed = max(1, used // 4)
        passed = fixed + (places - fixed + offset_by * (used - fixed)) % max(1, number_of - fixed)
        return jnp.zeros((number_of,), jnp.int32).at[sequence[jnp.where(places < fixed, places, passed)]].set(jnp.asarray(sizes, jnp.int32))

    sizes = jnp.where(number % 4 == 0, named(crowded, number // 4), named(usual, number - number // 4 - 1))
    mixed = jax.random.permutation(jax.random.fold_in(own, 3), number_of)
    donor, sink = mixed[0:number_of // 2 * 2:2], mixed[1:number_of // 2 * 2:2]
    room = jnp.minimum(sizes[donor] - 1, limit - sizes[sink]) // 2
    room = jnp.where((donor == sequence[0]) | (sink == sequence[0]) | (sizes[sink] == 0), 0, jnp.maximum(room, 0))
    passed = jax.random.randint(jax.random.fold_in(own, 4), (number_of // 2,), 0, 1 << 20) % (room + 1)
    sizes = sizes.at[donor].add(-passed).at[sink].add(passed)
    members = jnp.searchsorted(jnp.cumsum(sizes), jnp.arange(rows * top), side="right").astype(jnp.int32)
    listing = members.reshape(top, rows).T
    listing = listing[jax.random.permutation(jax.random.fold_in(own, 1), rows)]
    offset_by = jax.random.randint(jax.random.fold_in(own, 2), (rows, 1), 0, top)
    return jnp.take_along_axis(listing, (jnp.arange(top)[None, :] + offset_by) % top, axis=1)


def shares(number_of, total, most, lean, full):
    weights = [(1 << 20) // math.isqrt(standing ** lean) + 1 for standing in range(1, number_of + 1)]
    largest = most if full else min(most, max(-(-total // number_of), total * weights[0] // sum(weights)))
    least = 1 if total - largest >= number_of - 1 else 0
    given, rest = [largest] + [least] * (number_of - 1), total - largest - least * (number_of - 1)
    while rest > 0:
        movable = [i for i in range(1, number_of) if given[i] < largest] or [i for i in range(1, number_of) if given[i] < most]
        pool, remaining = sum([weights[i] for i in movable]), rest
        for i in movable:
            extra = min(most - given[i], max(1, remaining * weights[i] // pool), rest)
            given[i] = given[i] + extra
            rest = rest - extra
    return np.array(given)


def gaussian(key, shape, spread, reach, split=(), held_as=jnp.bfloat16):
    gain = block_levels(key, shape, split, -0.22, 0.18) if split else 1.0
    values = jax.random.normal(key, shape, jnp.float32) * spread * gain
    return jnp.minimum(jnp.maximum(values, -reach), reach).astype(held_as)


def setup_inputs(seed: int = 0) -> dict:
    arg_keys = jax.random.split(jax.random.key(seed), 13)
    velocity = gaussian(arg_keys[0], (3, NZ, NY, NX), 1.0, 6.0, ((1, 8), (2, 4)), jnp.float32)
    slip = gaussian(arg_keys[1], (3, PARTS_SIZE), 1.0, 6.0, ((1, 32),), jnp.float32)
    rate = jnp.clip(jnp.exp(math.log(4.0) - 2.0794415 * jax.random.uniform(arg_keys[2], (PARTS_SIZE,), jnp.float32) ** block_levels(arg_keys[2], (PARTS_SIZE,), ((0, 32),), -0.2, 0.2)), 0.5, 4.0)
    owner_keys = jax.random.split(jax.random.fold_in(arg_keys[3], 1), PARTS_SIZE // P_DEV)
    owner_turns = jax.random.permutation(jax.random.fold_in(arg_keys[3], 3), PARTS_SIZE // P_DEV)
    owner = jax.vmap(lambda own, number: shared_out(jax.random.fold_in(arg_keys[3], 2), own, number, P_DEV, N_GZ, 1, CAP, 2))(owner_keys, owner_turns).reshape((PARTS_SIZE, 1))
    cell = place_ends(skewed_ids(arg_keys[4], (PARTS_SIZE,), CELLS_DEV, 1), jax.random.fold_in(arg_keys[4], 3), 0, CELLS_DEV - 1).astype(jnp.int32)
    count = place_ends(jax.random.randint(arg_keys[5], (N_GZ * N_GY,), P_DEV // 2, P_DEV + 1), jax.random.fold_in(arg_keys[5], 1), P_DEV // 2, P_DEV).astype(jnp.int32)
    w_in = gaussian(arg_keys[6], (F_IN, H), F_IN ** -0.5, 1.75)
    b_in = gaussian(arg_keys[7], (H,), 0.5, 3.0, (), jnp.float32)
    w_mid = gaussian(arg_keys[8], (H, H), H ** -0.5, 0.1875)
    b_mid = gaussian(arg_keys[9], (H,), 0.5, 3.0, (), jnp.float32)
    w_out = gaussian(arg_keys[10], (H, N_OUT), H ** -0.5, 0.1875)
    tau_bar = gaussian(arg_keys[11], (N_OUT, NZ, NY, NX), 0.25, 1.5, ((1, 8), (2, 4)))
    return {"velocity": velocity, "slip": slip, "rate": rate, "owner": owner, "cell": cell, "count": count, "w_in": w_in, "b_in": b_in, "w_mid": w_mid, "b_mid": b_mid, "w_out": w_out, "tau_bar": tau_bar}


def derive(field, axis):
    return (jnp.roll(field, -1, axis) - jnp.roll(field, 1, axis)) * 0.5


def dsilu(value):
    sig = jax.nn.sigmoid(value)
    return sig * (1.0 + value * (1.0 - sig))


def reference(velocity, slip, rate, owner, cell, count, w_in, b_in, w_mid, b_mid, w_out, tau_bar):
    slots = jnp.arange(PARTS_SIZE, dtype=jnp.int32)
    device = slots // P_DEV
    live = (slots % P_DEV) < count[device]
    ycol = device % N_GY
    zpos = owner[:, 0] * CZ + cell // (CY * NX)
    ypos = ycol * CY + (cell // NX) % CY
    xpos = cell % NX
    global_id = ((zpos * NY + ypos) * NX + xpos).astype(jnp.int32)
    force = jnp.where(live[None, :], rate[None, :] * slip, 0.0)
    source = jax.ops.segment_sum(force.T, global_id, NZ * NY * NX).T.reshape(3, NZ, NY, NX)
    grads = jnp.stack([derive(velocity[i], a) for i in range(3) for a in range(3)])
    feats = jnp.concatenate([grads, source], 0).astype(jnp.bfloat16)
    plane_feats = feats.transpose(1, 0, 2, 3).reshape(NZ, F_IN, NY * NX)
    plane_bar = tau_bar.transpose(1, 0, 2, 3).reshape(NZ, N_OUT, NY * NX)
    win = w_in.astype(jnp.float32)
    wmid = w_mid.astype(jnp.float32)
    wout = w_out.astype(jnp.float32)

    def plane(carry, inputs):
        gin, gbin, gmid, gbmid, gout = carry
        fts, tb = inputs
        ftf = fts.astype(jnp.float32)
        tbf = tb.astype(jnp.float32)
        pre1 = jnp.einsum('fh,fc->hc', win, ftf) + b_in[:, None]
        h1 = jax.nn.silu(pre1).astype(jnp.bfloat16)
        h1f = h1.astype(jnp.float32)
        pre2 = jnp.einsum('gh,gc->hc', wmid, h1f) + b_mid[:, None]
        h2 = jax.nn.silu(pre2).astype(jnp.bfloat16)
        h2f = h2.astype(jnp.float32)
        stress = jnp.einsum('ho,hc->oc', wout, h2f)
        gout = gout + jnp.einsum('hc,oc->ho', h2f, tbf)
        g2 = (jnp.einsum('ho,oc->hc', wout, tbf) * dsilu(pre2)).astype(jnp.bfloat16).astype(jnp.float32)
        gmid = gmid + jnp.einsum('gc,hc->gh', h1f, g2)
        gbmid = gbmid + jnp.sum(g2, 1)
        g1 = (jnp.einsum('gh,hc->gc', wmid, g2) * dsilu(pre1)).astype(jnp.bfloat16).astype(jnp.float32)
        gin = gin + jnp.einsum('fc,hc->fh', ftf, g1)
        gbin = gbin + jnp.sum(g1, 1)
        fbar = jnp.einsum('fh,hc->fc', win, g1)
        return (gin, gbin, gmid, gbmid, gout), (stress, fbar)

    init = (jnp.zeros((F_IN, H), jnp.float32), jnp.zeros((H,), jnp.float32),
            jnp.zeros((H, H), jnp.float32), jnp.zeros((H,), jnp.float32),
            jnp.zeros((H, N_OUT), jnp.float32))
    sums, planes = lax.scan(plane, init, (plane_feats, plane_bar))
    grad_w_in, grad_b_in, grad_w_mid, grad_b_mid, grad_w_out = sums
    stress = planes[0].reshape(NZ, N_OUT, NY, NX).transpose(1, 0, 2, 3)
    feats_bar = planes[1].reshape(NZ, F_IN, NY, NX).transpose(1, 0, 2, 3)
    velocity_bar = jnp.stack([-(derive(feats_bar[3 * i], 0) + derive(feats_bar[3 * i + 1], 1)
                                + derive(feats_bar[3 * i + 2], 2)) for i in range(3)])
    source_bar = feats_bar[9:12].reshape(3, NZ * NY * NX)
    back = source_bar[:, global_id]
    slip_bar = jnp.where(live[None, :], rate[None, :] * back, 0.0)
    rate_bar = jnp.where(live, jnp.sum(slip * back, 0), 0.0)
    return (stress, velocity_bar, slip_bar, rate_bar, grad_w_in, grad_b_in,
            grad_w_mid, grad_b_mid, grad_w_out)
```

```python
import jax
import jax.numpy as jnp
from jax import lax
from jax.sharding import PartitionSpec as P


def with_halo(cells, sides, width):
    for axis, dim in sides:
        count = lax.axis_size(axis)
        head = lax.slice_in_dim(cells, 0, width, axis=dim)
        tail = lax.slice_in_dim(cells, cells.shape[dim] - width, cells.shape[dim], axis=dim)
        cells = jnp.concatenate(
            [
                lax.ppermute(tail, axis, [(i, (i + 1) % count) for i in range(count)]),
                cells,
                lax.ppermute(head, axis, [((i + 1) % count, i) for i in range(count)]),
            ],
            axis=dim,
        )
    return cells


def dsilu(value):
    sig = jax.nn.sigmoid(value)
    return sig * (1.0 + value * (1.0 - sig))


def deposit(forces, cell_row, ncells):
    block = min(512, ncells)
    count_blocks = ncells // block

    def deposit_one_block(index):
        start = index * block
        onehot = (
            cell_row[0][:, None] == start + jnp.arange(block, dtype=jnp.int32)[None, :]
        ).astype(jnp.float32)
        return jnp.dot(
            forces, onehot, precision=lax.Precision.HIGHEST, preferred_element_type=jnp.float32
        )

    pieces = lax.map(deposit_one_block, jnp.arange(count_blocks, dtype=jnp.int32))
    return pieces.transpose(1, 0, 2).reshape(forces.shape[0], ncells)


def collect(values, cell_row, ncells):
    block = min(512, ncells)
    count_blocks = ncells // block

    def collect_one_block(index, total):
        start = index * block
        onehot = (
            start + jnp.arange(block, dtype=jnp.int32)[:, None] == cell_row[0][None, :]
        ).astype(jnp.float32)
        return total + jnp.dot(
            values, onehot, precision=lax.Precision.HIGHEST, preferred_element_type=jnp.float32
        )

    init = jnp.zeros((values.shape[0], cell_row.shape[1]), jnp.float32)
    return lax.fori_loop(0, count_blocks, collect_one_block, init)


def tree_dims(nz, ny):
    gy_bits = [("gy", b) for b in range((ny - 1).bit_length())]
    gz_bits = [("gz", b) for b in range((nz - 1).bit_length())]
    dims = gy_bits + gz_bits
    if len(gy_bits) < 2 or not gz_bits:
        return lambda index: dims
    first, second = [gy_bits[0], gy_bits[1], gz_bits[0]], [gy_bits[0], gz_bits[0], gy_bits[1]]
    rest = gy_bits[2:] + gz_bits[1:]
    return lambda index: (first if index % ny % 2 == 0 else second) + rest


def tree_allreduce(parts, nz, ny):
    orders = tree_dims(nz, ny)
    count = nz * ny
    steps = len(orders(0))

    def bit(index, dim):
        row, col = divmod(index, ny)
        return ((row if dim[0] == "gz" else col) >> dim[1]) & 1

    def partner(index, dim):
        row, col = divmod(index, ny)
        if dim[0] == "gz":
            row ^= 1 << dim[1]
        else:
            col ^= 1 << dim[1]
        return row * ny + col

    me = lax.axis_index("gz") * ny + lax.axis_index("gy")
    table = jnp.array([[bit(i, orders(i)[k]) for k in range(steps)] for i in range(count)], jnp.int32)
    mine = table[me]
    pairs = [[(i, partner(i, orders(i)[k])) for i in range(count)] for k in range(steps)]
    for k in range(steps):
        half = parts[0].shape[0] // 2
        keep = [lax.dynamic_slice_in_dim(p, mine[k] * half, half, 0) for p in parts]
        send = [lax.dynamic_slice_in_dim(p, (1 - mine[k]) * half, half, 0) for p in parts]
        got = lax.ppermute(send, ("gz", "gy"), pairs[k])
        parts = [a + b for a, b in zip(keep, got)]
    for k in reversed(range(steps)):
        got = lax.ppermute(parts, ("gz", "gy"), pairs[k])
        low = mine[k] == 0
        parts = [
            jnp.concatenate([jnp.where(low, a, b), jnp.where(low, b, a)], 0)
            for a, b in zip(parts, got)
        ]
    return parts


def roll_diff(field):
    return (jnp.roll(field, -1, 3) - jnp.roll(field, 1, 3)) * 0.5


def shards(velocity, slip, rate, owner, cell, count, w_in, b_in, w_mid, b_mid, w_out, tau_bar):
    nparts = slip.shape[1]
    slabs = lax.axis_size("gz")
    capacity = 2 * nparts // slabs
    width_all = slabs * capacity
    ncz, ncy, ncx = (velocity.shape[1], velocity.shape[2], velocity.shape[3])
    ncells = ncz * ncy * ncx
    padded = with_halo(velocity, (("gz", 1), ("gy", 2)), 1)
    core = padded[:, 1:-1, 1:-1]
    along_z = (padded[:, 2:, 1:-1] - padded[:, :-2, 1:-1]) * 0.5
    along_y = (padded[:, 1:-1, 2:] - padded[:, 1:-1, :-2]) * 0.5
    grads = jnp.stack([along_z, along_y, roll_diff(core)], 1).reshape(9, ncells)
    live = jnp.arange(nparts, dtype=jnp.int32) < count[0]
    force = jnp.where(live[None, :], rate[None, :] * slip, 0.0)
    owners = owner[:, 0]
    member = (owners[:, None] == jnp.arange(slabs, dtype=jnp.int32)[None, :]).astype(jnp.int32)
    before = jnp.cumsum(member, 0) - member
    position = jnp.sum(before * member, 1)
    slot = owners * capacity + position
    send_force = jnp.zeros((3, width_all), jnp.float32).at[:, slot].set(force)
    send_cell = jnp.full((1, width_all), -1, jnp.int32).at[0, slot].set(jnp.where(live, cell, -1))
    recv_force, recv_cell = (
        lax.all_to_all(send_force, "gz", split_axis=1, concat_axis=1, tiled=True),
        lax.all_to_all(send_cell, "gz", split_axis=1, concat_axis=1, tiled=True),
    )
    source = deposit(recv_force, recv_cell, ncells)
    feats = jnp.concatenate([grads, source], 0).astype(jnp.bfloat16)
    tbar = tau_bar.reshape(tau_bar.shape[0], ncells)
    pre1 = jnp.einsum("fh,fc->hc", w_in, feats, preferred_element_type=jnp.float32) + b_in[:, None]
    hidden_one = jax.nn.silu(pre1).astype(jnp.bfloat16)
    pre2 = (
        jnp.einsum("gh,gc->hc", w_mid, hidden_one, preferred_element_type=jnp.float32)
        + b_mid[:, None]
    )
    hidden_two = jax.nn.silu(pre2).astype(jnp.bfloat16)
    stress = jnp.einsum("ho,hc->oc", w_out, hidden_two, preferred_element_type=jnp.float32)
    grad_w_out = jnp.einsum("hc,oc->ho", hidden_two, tbar, preferred_element_type=jnp.float32)
    back_two = jnp.einsum("ho,oc->hc", w_out, tbar, preferred_element_type=jnp.float32)
    delta_two = (back_two * dsilu(pre2)).astype(jnp.bfloat16)
    grad_w_mid = jnp.einsum("gc,hc->gh", hidden_one, delta_two, preferred_element_type=jnp.float32)
    grad_b_mid = jnp.sum(delta_two.astype(jnp.float32), 1)
    back_one = jnp.einsum("gh,hc->gc", w_mid, delta_two, preferred_element_type=jnp.float32)
    delta_one = (back_one * dsilu(pre1)).astype(jnp.bfloat16)
    grad_w_in = jnp.einsum("fc,hc->fh", feats, delta_one, preferred_element_type=jnp.float32)
    grad_b_in = jnp.sum(delta_one.astype(jnp.float32), 1)
    nz, ny = lax.axis_size("gz"), lax.axis_size("gy")
    count = nz * ny
    small = jnp.concatenate(
        [grad_w_in.reshape(-1), grad_b_in, grad_b_mid, grad_w_out.reshape(-1)]
    )
    width = -(-small.shape[0] // count)
    small_pad = jnp.pad(small, (0, width * count - small.shape[0])).reshape(count, width)
    big = grad_w_mid.reshape(count, -1, grad_w_mid.shape[1])
    big, small_pad = tree_allreduce([big, small_pad], nz, ny)
    grad_w_mid = big.reshape(grad_w_mid.shape)
    small = small_pad.reshape(-1)
    sizes = [grad_w_in.size, grad_b_in.size, grad_b_mid.size, grad_w_out.size]
    offsets = [0, sizes[0], sizes[0] + sizes[1], sizes[0] + sizes[1] + sizes[2]]
    grad_w_in = small[offsets[0] : offsets[0] + sizes[0]].reshape(grad_w_in.shape)
    grad_b_in = small[offsets[1] : offsets[1] + sizes[1]]
    grad_b_mid = small[offsets[2] : offsets[2] + sizes[2]]
    grad_w_out = small[offsets[3] : offsets[3] + sizes[3]].reshape(grad_w_out.shape)
    feats_bar = jnp.einsum("fh,hc->fc", w_in, delta_one, preferred_element_type=jnp.float32)
    grads_bar = feats_bar[:9].reshape(3, 3, ncz, ncy, ncx)
    zpad = with_halo(grads_bar[:, 0], (("gz", 1),), 1)
    ypad = with_halo(grads_bar[:, 1], (("gy", 2),), 1)
    term_z = (zpad[:, 2:] - zpad[:, :-2]) * 0.5
    term_y = (ypad[:, :, 2:] - ypad[:, :, :-2]) * 0.5
    term_x = roll_diff(grads_bar[:, 2])
    velocity_bar = -(term_z + term_y + term_x)
    source_bar = feats_bar[9:12]
    per_slot = collect(source_bar, recv_cell, ncells)
    returned = lax.all_to_all(per_slot, "gz", split_axis=1, concat_axis=1, tiled=True)
    at_particle = returned[:, slot]
    slip_bar = jnp.where(live[None, :], rate[None, :] * at_particle, 0.0)
    rate_bar = jnp.where(live, jnp.sum(slip * at_particle, 0), 0.0)
    return (
        stress.reshape(stress.shape[0], ncz, ncy, ncx),
        velocity_bar,
        slip_bar,
        rate_bar,
        grad_w_in,
        grad_b_in,
        grad_w_mid,
        grad_b_mid,
        grad_w_out,
    )


def solution(mesh):
    return jax.shard_map(
        shards,
        mesh=mesh,
        in_specs=(
            P(None, "gz", "gy", None),
            P(None, ("gz", "gy")),
            P(("gz", "gy")),
            P(("gz", "gy"), None),
            P(("gz", "gy")),
            P(("gz", "gy")),
            P(),
            P(),
            P(),
            P(),
            P(),
            P(None, "gz", "gy", None),
        ),
        out_specs=(
            P(None, "gz", "gy", None),
            P(None, "gz", "gy", None),
            P(None, ("gz", "gy")),
            P(("gz", "gy")),
            P(),
            P(),
            P(),
            P(),
            P(),
        ),
        check_vma=False,
    )
```

```python
import jax
import jax.numpy as jnp
from jax import lax
from jax.sharding import PartitionSpec as P


def with_halo(cells, sides, width):
    for axis, dim in sides:
        count = lax.axis_size(axis)
        head = lax.slice_in_dim(cells, 0, width, axis=dim)
        tail = lax.slice_in_dim(cells, cells.shape[dim] - width, cells.shape[dim], axis=dim)
        cells = jnp.concatenate(
            [
                lax.ppermute(tail, axis, [(i, (i + 1) % count) for i in range(count)]),
                cells,
                lax.ppermute(head, axis, [((i + 1) % count, i) for i in range(count)]),
            ],
            axis=dim,
        )
    return cells


def dsilu(value):
    sig = jax.nn.sigmoid(value)
    return sig * (1.0 + value * (1.0 - sig))


def deposit(forces, cell_row, ncells):
    block = min(512, ncells)
    count_blocks = ncells // block

    def deposit_one_block(index):
        start = index * block
        onehot = (
            cell_row[0][:, None] == start + jnp.arange(block, dtype=jnp.int32)[None, :]
        ).astype(jnp.float32)
        return jnp.dot(
            forces, onehot, precision=lax.Precision.HIGHEST, preferred_element_type=jnp.float32
        )

    pieces = lax.map(deposit_one_block, jnp.arange(count_blocks, dtype=jnp.int32))
    return pieces.transpose(1, 0, 2).reshape(forces.shape[0], ncells)


def collect(values, cell_row, ncells):
    block = min(512, ncells)
    count_blocks = ncells // block

    def collect_one_block(index, total):
        start = index * block
        onehot = (
            start + jnp.arange(block, dtype=jnp.int32)[:, None] == cell_row[0][None, :]
        ).astype(jnp.float32)
        return total + jnp.dot(
            values, onehot, precision=lax.Precision.HIGHEST, preferred_element_type=jnp.float32
        )

    init = jnp.zeros((values.shape[0], cell_row.shape[1]), jnp.float32)
    return lax.fori_loop(0, count_blocks, collect_one_block, init)


def tree_dims(nz, ny):
    gy_bits = [("gy", b) for b in range((ny - 1).bit_length())]
    gz_bits = [("gz", b) for b in range((nz - 1).bit_length())]
    dims = gy_bits + gz_bits
    if len(gy_bits) < 2 or not gz_bits:
        return lambda index: dims
    first, second = [gy_bits[0], gy_bits[1], gz_bits[0]], [gy_bits[0], gz_bits[0], gy_bits[1]]
    rest = gy_bits[2:] + gz_bits[1:]
    return lambda index: (first if index % ny % 2 == 0 else second) + rest


def tree_allreduce(parts, nz, ny):
    orders = tree_dims(nz, ny)
    count = nz * ny
    steps = len(orders(0))

    def bit(index, dim):
        row, col = divmod(index, ny)
        return ((row if dim[0] == "gz" else col) >> dim[1]) & 1

    def partner(index, dim):
        row, col = divmod(index, ny)
        if dim[0] == "gz":
            row ^= 1 << dim[1]
        else:
            col ^= 1 << dim[1]
        return row * ny + col

    me = lax.axis_index("gz") * ny + lax.axis_index("gy")
    table = jnp.array([[bit(i, orders(i)[k]) for k in range(steps)] for i in range(count)], jnp.int32)
    mine = table[me]
    pairs = [[(i, partner(i, orders(i)[k])) for i in range(count)] for k in range(steps)]
    for k in range(steps):
        half = parts[0].shape[0] // 2
        keep = [lax.dynamic_slice_in_dim(p, mine[k] * half, half, 0) for p in parts]
        send = [lax.dynamic_slice_in_dim(p, (1 - mine[k]) * half, half, 0) for p in parts]
        got = lax.ppermute(send, ("gz", "gy"), pairs[k])
        parts = [a + b for a, b in zip(keep, got)]
    for k in reversed(range(steps)):
        got = lax.ppermute(parts, ("gz", "gy"), pairs[k])
        low = mine[k] == 0
        parts = [
            jnp.concatenate([jnp.where(low, a, b), jnp.where(low, b, a)], 0)
            for a, b in zip(parts, got)
        ]
    return parts


def roll_diff(field):
    return (jnp.roll(field, -1, 3) - jnp.roll(field, 1, 3)) * 0.5


def shards(velocity, slip, rate, owner, cell, count, w_in, b_in, w_mid, b_mid, w_out, tau_bar):
    nparts = slip.shape[1]
    slabs = lax.axis_size("gz")
    capacity = 2 * nparts // slabs
    width_all = slabs * capacity
    ncz, ncy, ncx = (velocity.shape[1], velocity.shape[2], velocity.shape[3])
    ncells = ncz * ncy * ncx
    padded = with_halo(velocity, (("gz", 1), ("gy", 2)), 1)
    core = padded[:, 1:-1, 1:-1]
    along_z = (padded[:, 2:, 1:-1] - padded[:, :-2, 1:-1]) * 0.5
    along_y = (padded[:, 1:-1, 2:] - padded[:, 1:-1, :-2]) * 0.5
    grads = jnp.stack([along_z, along_y, roll_diff(core)], 1).reshape(9, ncells)
    live = jnp.arange(nparts, dtype=jnp.int32) < count[0]
    force = jnp.where(live[None, :], rate[None, :] * slip, 0.0)
    owners = owner[:, 0]
    member = (owners[:, None] == jnp.arange(slabs, dtype=jnp.int32)[None, :]).astype(jnp.int32)
    before = jnp.cumsum(member, 0) - member
    position = jnp.sum(before * member, 1)
    slot = owners * capacity + position
    send_force = jnp.zeros((3, width_all), jnp.float32).at[:, slot].set(force)
    send_cell = jnp.full((1, width_all), -1, jnp.int32).at[0, slot].set(jnp.where(live, cell, -1))
    recv_force, recv_cell = (
        lax.all_to_all(send_force, "gz", split_axis=1, concat_axis=1, tiled=True),
        lax.all_to_all(send_cell, "gz", split_axis=1, concat_axis=1, tiled=True),
    )
    source = deposit(recv_force, recv_cell, ncells)
    feats = jnp.concatenate([grads, source], 0).astype(jnp.bfloat16)
    tbar = tau_bar.reshape(tau_bar.shape[0], ncells)
    pre1 = jnp.einsum("fh,fc->hc", w_in, feats, preferred_element_type=jnp.float32) + b_in[:, None]
    hidden_one = jax.nn.silu(pre1).astype(jnp.bfloat16)
    pre2 = (
        jnp.einsum("gh,gc->hc", w_mid, hidden_one, preferred_element_type=jnp.float32)
        + b_mid[:, None]
    )
    hidden_two = jax.nn.silu(pre2).astype(jnp.bfloat16)
    stress = jnp.einsum("ho,hc->oc", w_out, hidden_two, preferred_element_type=jnp.float32)
    grad_w_out = jnp.einsum("hc,oc->ho", hidden_two, tbar, preferred_element_type=jnp.float32)
    back_two = jnp.einsum("ho,oc->hc", w_out, tbar, preferred_element_type=jnp.float32)
    delta_two = (back_two * dsilu(pre2)).astype(jnp.bfloat16)
    grad_w_mid = jnp.einsum("gc,hc->gh", hidden_one, delta_two, preferred_element_type=jnp.float32)
    grad_b_mid = jnp.sum(delta_two.astype(jnp.float32), 1)
    back_one = jnp.einsum("gh,hc->gc", w_mid, delta_two, preferred_element_type=jnp.float32)
    delta_one = (back_one * dsilu(pre1)).astype(jnp.bfloat16)
    grad_w_in = jnp.einsum("fc,hc->fh", feats, delta_one, preferred_element_type=jnp.float32)
    grad_b_in = jnp.sum(delta_one.astype(jnp.float32), 1)
    nz, ny = lax.axis_size("gz"), lax.axis_size("gy")
    count = nz * ny
    small = jnp.concatenate(
        [grad_w_in.reshape(-1), grad_b_in, grad_b_mid, grad_w_out.reshape(-1)]
    )
    lanes = grad_w_mid.shape[1]
    rows = grad_w_mid.shape[0] // count
    extra = -(-small.shape[0] // (count * lanes))
    small_pad = jnp.pad(small, (0, extra * count * lanes - small.shape[0]))
    packed = jnp.concatenate(
        [grad_w_mid.reshape(count, rows, lanes), small_pad.reshape(count, extra, lanes)], 1
    )
    (packed,) = tree_allreduce([packed], nz, ny)
    grad_w_mid = packed[:, :rows].reshape(grad_w_mid.shape)
    small = packed[:, rows:].reshape(-1)
    sizes = [grad_w_in.size, grad_b_in.size, grad_b_mid.size, grad_w_out.size]
    offsets = [0, sizes[0], sizes[0] + sizes[1], sizes[0] + sizes[1] + sizes[2]]
    grad_w_in = small[offsets[0] : offsets[0] + sizes[0]].reshape(grad_w_in.shape)
    grad_b_in = small[offsets[1] : offsets[1] + sizes[1]]
    grad_b_mid = small[offsets[2] : offsets[2] + sizes[2]]
    grad_w_out = small[offsets[3] : offsets[3] + sizes[3]].reshape(grad_w_out.shape)
    feats_bar = jnp.einsum("fh,hc->fc", w_in, delta_one, preferred_element_type=jnp.float32)
    grads_bar = feats_bar[:9].reshape(3, 3, ncz, ncy, ncx)
    zpad = with_halo(grads_bar[:, 0], (("gz", 1),), 1)
    ypad = with_halo(grads_bar[:, 1], (("gy", 2),), 1)
    term_z = (zpad[:, 2:] - zpad[:, :-2]) * 0.5
    term_y = (ypad[:, :, 2:] - ypad[:, :, :-2]) * 0.5
    term_x = roll_diff(grads_bar[:, 2])
    velocity_bar = -(term_z + term_y + term_x)
    source_bar = feats_bar[9:12]
    per_slot = collect(source_bar, recv_cell, ncells)
    returned = lax.all_to_all(per_slot, "gz", split_axis=1, concat_axis=1, tiled=True)
    at_particle = returned[:, slot]
    slip_bar = jnp.where(live[None, :], rate[None, :] * at_particle, 0.0)
    rate_bar = jnp.where(live, jnp.sum(slip * at_particle, 0), 0.0)
    return (
        stress.reshape(stress.shape[0], ncz, ncy, ncx),
        velocity_bar,
        slip_bar,
        rate_bar,
        grad_w_in,
        grad_b_in,
        grad_w_mid,
        grad_b_mid,
        grad_w_out,
    )


def solution(mesh):
    return jax.shard_map(
        shards,
        mesh=mesh,
        in_specs=(
            P(None, "gz", "gy", None),
            P(None, ("gz", "gy")),
            P(("gz", "gy")),
            P(("gz", "gy"), None),
            P(("gz", "gy")),
            P(("gz", "gy")),
            P(),
            P(),
            P(),
            P(),
            P(),
            P(None, "gz", "gy", None),
        ),
        out_specs=(
            P(None, "gz", "gy", None),
            P(None, "gz", "gy", None),
            P(None, ("gz", "gy")),
            P(("gz", "gy")),
            P(),
            P(),
            P(),
            P(),
            P(),
        ),
        check_vma=False,
    )
```

```python
import jax
import jax.numpy as jnp
from jax import lax
from jax.sharding import PartitionSpec as P


def with_halo(cells, sides, width):
    for axis, dim in sides:
        count = lax.axis_size(axis)
        head = lax.slice_in_dim(cells, 0, width, axis=dim)
        tail = lax.slice_in_dim(cells, cells.shape[dim] - width, cells.shape[dim], axis=dim)
        cells = jnp.concatenate(
            [
                lax.ppermute(tail, axis, [(i, (i + 1) % count) for i in range(count)]),
                cells,
                lax.ppermute(head, axis, [((i + 1) % count, i) for i in range(count)]),
            ],
            axis=dim,
        )
    return cells


def dsilu(value):
    sig = jax.nn.sigmoid(value)
    return sig * (1.0 + value * (1.0 - sig))


def deposit(forces, cell_row, ncells):
    block = min(512, ncells)
    count_blocks = ncells // block

    def deposit_one_block(index):
        start = index * block
        onehot = (
            cell_row[0][:, None] == start + jnp.arange(block, dtype=jnp.int32)[None, :]
        ).astype(jnp.float32)
        return jnp.dot(
            forces, onehot, precision=lax.Precision.HIGHEST, preferred_element_type=jnp.float32
        )

    pieces = lax.map(deposit_one_block, jnp.arange(count_blocks, dtype=jnp.int32))
    return pieces.transpose(1, 0, 2).reshape(forces.shape[0], ncells)


def collect(values, cell_row, ncells):
    block = min(512, ncells)
    count_blocks = ncells // block

    def collect_one_block(index, total):
        start = index * block
        onehot = (
            start + jnp.arange(block, dtype=jnp.int32)[:, None] == cell_row[0][None, :]
        ).astype(jnp.float32)
        return total + jnp.dot(
            values, onehot, precision=lax.Precision.HIGHEST, preferred_element_type=jnp.float32
        )

    init = jnp.zeros((values.shape[0], cell_row.shape[1]), jnp.float32)
    return lax.fori_loop(0, count_blocks, collect_one_block, init)


def tree_dims(nz, ny):
    gy_bits = [("gy", b) for b in range((ny - 1).bit_length())]
    gz_bits = [("gz", b) for b in range((nz - 1).bit_length())]
    dims = gy_bits + gz_bits
    if len(gy_bits) < 2 or not gz_bits:
        return lambda index: dims
    first, second = [gy_bits[0], gy_bits[1], gz_bits[0]], [gy_bits[0], gz_bits[0], gy_bits[1]]
    rest = gy_bits[2:] + gz_bits[1:]
    return lambda index: (first if index % ny % 2 == 0 else second) + rest


def tree_allreduce(packed, nz, ny, windows):
    orders = tree_dims(nz, ny)
    count = nz * ny
    steps = len(orders(0))
    lane_steps = min(steps, 3)

    def bit(index, dim):
        row, col = divmod(index, ny)
        return ((row if dim[0] == "gz" else col) >> dim[1]) & 1

    def partner(index, dim):
        row, col = divmod(index, ny)
        if dim[0] == "gz":
            row ^= 1 << dim[1]
        else:
            col ^= 1 << dim[1]
        return row * ny + col

    me = lax.axis_index("gz") * ny + lax.axis_index("gy")
    table = jnp.array([[bit(i, orders(i)[k]) for k in range(steps)] for i in range(count)], jnp.int32)
    mine = table[me]
    pairs = [[(i, partner(i, orders(i)[k])) for i in range(count)] for k in range(steps)]
    results = {}

    def exchange(send, k, key):
        if key not in windows:
            return lax.ppermute(send, ("gz", "gy"), pairs[k])
        work, inputs = windows[key]
        send, inputs = lax.optimization_barrier((send, inputs))
        got = lax.ppermute(send, ("gz", "gy"), pairs[k])
        outputs = work(*inputs)
        got, results[key] = lax.optimization_barrier((got, outputs))
        return got

    for k in range(steps):
        axis = 1 if k < lane_steps else 0
        half = packed.shape[axis] // 2
        keep = lax.dynamic_slice_in_dim(packed, mine[k] * half, half, axis)
        send = lax.dynamic_slice_in_dim(packed, (1 - mine[k]) * half, half, axis)
        packed = keep + exchange(send, k, k)
    for k in reversed(range(steps)):
        axis = 1 if k < lane_steps else 0
        got = exchange(packed, k, steps + k)
        low = mine[k] == 0
        packed = jnp.concatenate(
            [jnp.where(low, packed, got), jnp.where(low, got, packed)], axis
        )
    return packed, results


def roll_diff(field):
    return (jnp.roll(field, -1, 3) - jnp.roll(field, 1, 3)) * 0.5


def shards(velocity, slip, rate, owner, cell, count, w_in, b_in, w_mid, b_mid, w_out, tau_bar):
    nparts = slip.shape[1]
    slabs = lax.axis_size("gz")
    capacity = 2 * nparts // slabs
    width_all = slabs * capacity
    ncz, ncy, ncx = (velocity.shape[1], velocity.shape[2], velocity.shape[3])
    ncells = ncz * ncy * ncx
    padded = with_halo(velocity, (("gz", 1), ("gy", 2)), 1)
    core = padded[:, 1:-1, 1:-1]
    along_z = (padded[:, 2:, 1:-1] - padded[:, :-2, 1:-1]) * 0.5
    along_y = (padded[:, 1:-1, 2:] - padded[:, 1:-1, :-2]) * 0.5
    grads = jnp.stack([along_z, along_y, roll_diff(core)], 1).reshape(9, ncells)
    live = jnp.arange(nparts, dtype=jnp.int32) < count[0]
    force = jnp.where(live[None, :], rate[None, :] * slip, 0.0)
    owners = owner[:, 0]
    member = (owners[:, None] == jnp.arange(slabs, dtype=jnp.int32)[None, :]).astype(jnp.int32)
    before = jnp.cumsum(member, 0) - member
    position = jnp.sum(before * member, 1)
    slot = owners * capacity + position
    send_force = jnp.zeros((3, width_all), jnp.float32).at[:, slot].set(force)
    send_cell = jnp.full((1, width_all), -1, jnp.int32).at[0, slot].set(jnp.where(live, cell, -1))
    recv_force, recv_cell = (
        lax.all_to_all(send_force, "gz", split_axis=1, concat_axis=1, tiled=True),
        lax.all_to_all(send_cell, "gz", split_axis=1, concat_axis=1, tiled=True),
    )
    source = deposit(recv_force, recv_cell, ncells)
    feats = jnp.concatenate([grads, source], 0).astype(jnp.bfloat16)
    tbar = tau_bar.reshape(tau_bar.shape[0], ncells)
    pre1 = jnp.einsum("fh,fc->hc", w_in, feats, preferred_element_type=jnp.float32) + b_in[:, None]
    hidden_one = jax.nn.silu(pre1).astype(jnp.bfloat16)
    pre2 = (
        jnp.einsum("gh,gc->hc", w_mid, hidden_one, preferred_element_type=jnp.float32)
        + b_mid[:, None]
    )
    hidden_two = jax.nn.silu(pre2).astype(jnp.bfloat16)
    stress = jnp.einsum("ho,hc->oc", w_out, hidden_two, preferred_element_type=jnp.float32)
    grad_w_out_t = jnp.einsum("oc,hc->oh", tbar, hidden_two, preferred_element_type=jnp.float32)
    back_two = jnp.einsum("ho,oc->hc", w_out, tbar, preferred_element_type=jnp.float32)
    delta_two = (back_two * dsilu(pre2)).astype(jnp.bfloat16)
    back_one = jnp.einsum("gh,hc->gc", w_mid, delta_two, preferred_element_type=jnp.float32)
    delta_one = (back_one * dsilu(pre1)).astype(jnp.bfloat16)
    grad_w_in = jnp.einsum("fc,hc->fh", feats, delta_one, preferred_element_type=jnp.float32)
    grad_b_in = jnp.sum(delta_one.astype(jnp.float32), 1)
    nz, ny = lax.axis_size("gz"), lax.axis_size("gy")
    count = nz * ny
    feats_bar = jnp.einsum("fh,hc->fc", w_in, delta_one, preferred_element_type=jnp.float32)

    def velocity_work(feats_bar):
        grads_bar = feats_bar[:9].reshape(3, 3, ncz, ncy, ncx)
        zpad = with_halo(grads_bar[:, 0], (("gz", 1),), 1)
        ypad = with_halo(grads_bar[:, 1], (("gy", 2),), 1)
        term_z = (zpad[:, 2:] - zpad[:, :-2]) * 0.5
        term_y = (ypad[:, :, 2:] - ypad[:, :, :-2]) * 0.5
        term_x = roll_diff(grads_bar[:, 2])
        return -(term_z + term_y + term_x)

    def particle_work(feats_bar, recv_cell, slot, live, rate, slip):
        per_slot = collect(feats_bar[9:12], recv_cell, ncells)
        returned = lax.all_to_all(per_slot, "gz", split_axis=1, concat_axis=1, tiled=True)
        at_particle = returned[:, slot]
        slip_bar = jnp.where(live[None, :], rate[None, :] * at_particle, 0.0)
        rate_bar = jnp.where(live, jnp.sum(slip * at_particle, 0), 0.0)
        return slip_bar, rate_bar

    steps = (count - 1).bit_length()
    row_steps = max(steps - 3, 0)
    nh = hidden_one.shape[0]
    small = jnp.concatenate([grad_w_in, grad_b_in[None], grad_w_out_t], 0)
    rows_needed = nh + 1 + small.shape[0]
    unit = 8 << row_steps
    rows_total = -(-rows_needed // unit) * unit
    left = jnp.concatenate(
        [
            hidden_one,
            jnp.ones((1, ncells), hidden_one.dtype),
            jnp.zeros((rows_total - nh - 1, ncells), hidden_one.dtype),
        ],
        0,
    )
    packed = jnp.einsum("gc,hc->gh", left, delta_two, preferred_element_type=jnp.float32)
    packed = lax.dynamic_update_slice(packed, small, (nh + 1, 0))
    windows = {
        1: (particle_work, (feats_bar, recv_cell, slot, live, rate, slip)),
        2: (velocity_work, (feats_bar,)),
    }
    packed, results = tree_allreduce(packed, nz, ny, windows)
    slip_bar, rate_bar = results[1]
    velocity_bar = results[2]
    grad_w_mid = packed[:nh]
    grad_b_mid = packed[nh]
    grad_w_in = packed[nh + 1 : nh + 1 + grad_w_in.shape[0]]
    start = nh + 1 + grad_w_in.shape[0]
    grad_b_in = packed[start]
    grad_w_out = packed[start + 1 : start + 1 + grad_w_out_t.shape[0]].T
    return (
        stress.reshape(stress.shape[0], ncz, ncy, ncx),
        velocity_bar,
        slip_bar,
        rate_bar,
        grad_w_in,
        grad_b_in,
        grad_w_mid,
        grad_b_mid,
        grad_w_out,
    )


def solution(mesh):
    return jax.shard_map(
        shards,
        mesh=mesh,
        in_specs=(
            P(None, "gz", "gy", None),
            P(None, ("gz", "gy")),
            P(("gz", "gy")),
            P(("gz", "gy"), None),
            P(("gz", "gy")),
            P(("gz", "gy")),
            P(),
            P(),
            P(),
            P(),
            P(),
            P(None, "gz", "gy", None),
        ),
        out_specs=(
            P(None, "gz", "gy", None),
            P(None, "gz", "gy", None),
            P(None, ("gz", "gy")),
            P(("gz", "gy")),
            P(),
            P(),
            P(),
            P(),
            P(),
        ),
        check_vma=False,
    )
```

```python
import jax
import jax.numpy as jnp
from jax import lax
from jax.sharding import PartitionSpec as P


def with_halo(cells, sides, width):
    for axis, dim in sides:
        count = lax.axis_size(axis)
        head = lax.slice_in_dim(cells, 0, width, axis=dim)
        tail = lax.slice_in_dim(cells, cells.shape[dim] - width, cells.shape[dim], axis=dim)
        cells = jnp.concatenate(
            [
                lax.ppermute(tail, axis, [(i, (i + 1) % count) for i in range(count)]),
                cells,
                lax.ppermute(head, axis, [((i + 1) % count, i) for i in range(count)]),
            ],
            axis=dim,
        )
    return cells


def dsilu(value):
    sig = jax.nn.sigmoid(value)
    return sig * (1.0 + value * (1.0 - sig))


def deposit(forces, cell_row, ncells):
    block = min(512, ncells)
    count_blocks = ncells // block

    def deposit_one_block(index):
        start = index * block
        onehot = (
            cell_row[0][:, None] == start + jnp.arange(block, dtype=jnp.int32)[None, :]
        ).astype(jnp.float32)
        return jnp.dot(
            forces, onehot, precision=lax.Precision.HIGHEST, preferred_element_type=jnp.float32
        )

    pieces = lax.map(deposit_one_block, jnp.arange(count_blocks, dtype=jnp.int32))
    return pieces.transpose(1, 0, 2).reshape(forces.shape[0], ncells)


def collect(values, cell_row, ncells):
    block = min(512, ncells)
    count_blocks = ncells // block

    def collect_one_block(index, total):
        start = index * block
        onehot = (
            start + jnp.arange(block, dtype=jnp.int32)[:, None] == cell_row[0][None, :]
        ).astype(jnp.float32)
        return total + jnp.dot(
            values, onehot, precision=lax.Precision.HIGHEST, preferred_element_type=jnp.float32
        )

    init = jnp.zeros((values.shape[0], cell_row.shape[1]), jnp.float32)
    return lax.fori_loop(0, count_blocks, collect_one_block, init)


def tree_dims(nz, ny):
    gy_bits = [("gy", b) for b in range((ny - 1).bit_length())]
    gz_bits = [("gz", b) for b in range((nz - 1).bit_length())]
    dims = gy_bits + gz_bits
    if len(gy_bits) < 2 or not gz_bits:
        return lambda index: dims
    first, second = [gy_bits[0], gy_bits[1], gz_bits[0]], [gy_bits[0], gz_bits[0], gy_bits[1]]
    rest = gy_bits[2:] + gz_bits[1:]
    return lambda index: (first if index % ny % 2 == 0 else second) + rest


def tree_allreduce(packed, nz, ny, windows):
    orders = tree_dims(nz, ny)
    count = nz * ny
    steps = len(orders(0))
    lane_steps = min(steps, 3)

    def bit(index, dim):
        row, col = divmod(index, ny)
        return ((row if dim[0] == "gz" else col) >> dim[1]) & 1

    def partner(index, dim):
        row, col = divmod(index, ny)
        if dim[0] == "gz":
            row ^= 1 << dim[1]
        else:
            col ^= 1 << dim[1]
        return row * ny + col

    me = lax.axis_index("gz") * ny + lax.axis_index("gy")
    table = jnp.array([[bit(i, orders(i)[k]) for k in range(steps)] for i in range(count)], jnp.int32)
    mine = table[me]
    pairs = [[(i, partner(i, orders(i)[k])) for i in range(count)] for k in range(steps)]
    results = {}

    def exchange(send, k, key):
        if key not in windows:
            return lax.ppermute(send, ("gz", "gy"), pairs[k])
        work, inputs = windows[key]
        send, inputs = lax.optimization_barrier((send, inputs))
        got = lax.ppermute(send, ("gz", "gy"), pairs[k])
        outputs = work(*inputs)
        got, results[key] = lax.optimization_barrier((got, outputs))
        return got

    for k in range(steps):
        axis = 1 if k < lane_steps else 0
        half = packed.shape[axis] // 2
        keep = lax.dynamic_slice_in_dim(packed, mine[k] * half, half, axis)
        send = lax.dynamic_slice_in_dim(packed, (1 - mine[k]) * half, half, axis)
        packed = keep + exchange(send, k, k)
    for k in reversed(range(steps)):
        axis = 1 if k < lane_steps else 0
        got = exchange(packed, k, steps + k)
        low = mine[k] == 0
        packed = jnp.concatenate(
            [jnp.where(low, packed, got), jnp.where(low, got, packed)], axis
        )
    return packed, results


def roll_diff(field):
    return (jnp.roll(field, -1, 3) - jnp.roll(field, 1, 3)) * 0.5


def shards(velocity, slip, rate, owner, cell, count, w_in, b_in, w_mid, b_mid, w_out, tau_bar):
    nparts = slip.shape[1]
    slabs = lax.axis_size("gz")
    capacity = 2 * nparts // slabs
    width_all = slabs * capacity
    ncz, ncy, ncx = (velocity.shape[1], velocity.shape[2], velocity.shape[3])
    ncells = ncz * ncy * ncx
    padded = with_halo(velocity, (("gz", 1), ("gy", 2)), 1)
    core = padded[:, 1:-1, 1:-1]
    along_z = (padded[:, 2:, 1:-1] - padded[:, :-2, 1:-1]) * 0.5
    along_y = (padded[:, 1:-1, 2:] - padded[:, 1:-1, :-2]) * 0.5
    grads = jnp.stack([along_z, along_y, roll_diff(core)], 1).reshape(9, ncells)
    live = jnp.arange(nparts, dtype=jnp.int32) < count[0]
    force = jnp.where(live[None, :], rate[None, :] * slip, 0.0)
    owners = owner[:, 0]
    member = (owners[:, None] == jnp.arange(slabs, dtype=jnp.int32)[None, :]).astype(jnp.int32)
    before = jnp.cumsum(member, 0) - member
    position = jnp.sum(before * member, 1)
    slot = owners * capacity + position
    payload = jnp.concatenate(
        [force, jnp.where(live, cell, -1).astype(jnp.float32)[None]], 0
    )
    base = jnp.concatenate(
        [jnp.zeros((3, width_all), jnp.float32), jnp.full((1, width_all), -1.0, jnp.float32)], 0
    )
    received = lax.all_to_all(
        base.at[:, slot].set(payload), "gz", split_axis=1, concat_axis=1, tiled=True
    )
    recv_force = received[:3]
    recv_cell = received[3:].astype(jnp.int32)
    source = deposit(recv_force, recv_cell, ncells)
    feats = jnp.concatenate([grads, source], 0).astype(jnp.bfloat16)
    tbar = tau_bar.reshape(tau_bar.shape[0], ncells)
    pre1 = jnp.einsum("fh,fc->hc", w_in, feats, preferred_element_type=jnp.float32) + b_in[:, None]
    hidden_one = jax.nn.silu(pre1).astype(jnp.bfloat16)
    pre2 = (
        jnp.einsum("gh,gc->hc", w_mid, hidden_one, preferred_element_type=jnp.float32)
        + b_mid[:, None]
    )
    hidden_two = jax.nn.silu(pre2).astype(jnp.bfloat16)
    stress = jnp.einsum("ho,hc->oc", w_out, hidden_two, preferred_element_type=jnp.float32)
    grad_w_out_t = jnp.einsum("oc,hc->oh", tbar, hidden_two, preferred_element_type=jnp.float32)
    back_two = jnp.einsum("ho,oc->hc", w_out, tbar, preferred_element_type=jnp.float32)
    delta_two = (back_two * dsilu(pre2)).astype(jnp.bfloat16)
    back_one = jnp.einsum("gh,hc->gc", w_mid, delta_two, preferred_element_type=jnp.float32)
    delta_one = (back_one * dsilu(pre1)).astype(jnp.bfloat16)
    grad_w_in = jnp.einsum("fc,hc->fh", feats, delta_one, preferred_element_type=jnp.float32)
    grad_b_in = jnp.sum(delta_one.astype(jnp.float32), 1)
    nz, ny = lax.axis_size("gz"), lax.axis_size("gy")
    count = nz * ny
    feats_bar = jnp.einsum("fh,hc->fc", w_in, delta_one, preferred_element_type=jnp.float32)

    def velocity_work(feats_bar):
        grads_bar = feats_bar[:9].reshape(3, 3, ncz, ncy, ncx)
        zpad = with_halo(grads_bar[:, 0], (("gz", 1),), 1)
        ypad = with_halo(grads_bar[:, 1], (("gy", 2),), 1)
        term_z = (zpad[:, 2:] - zpad[:, :-2]) * 0.5
        term_y = (ypad[:, :, 2:] - ypad[:, :, :-2]) * 0.5
        term_x = roll_diff(grads_bar[:, 2])
        return -(term_z + term_y + term_x)

    def particle_work(feats_bar, recv_cell, slot, live, rate, slip):
        per_slot = collect(feats_bar[9:12], recv_cell, ncells)
        returned = lax.all_to_all(per_slot, "gz", split_axis=1, concat_axis=1, tiled=True)
        at_particle = returned[:, slot]
        slip_bar = jnp.where(live[None, :], rate[None, :] * at_particle, 0.0)
        rate_bar = jnp.where(live, jnp.sum(slip * at_particle, 0), 0.0)
        return slip_bar, rate_bar

    steps = (count - 1).bit_length()
    row_steps = max(steps - 3, 0)
    nh = hidden_one.shape[0]
    small = jnp.concatenate([grad_w_in, grad_b_in[None], grad_w_out_t], 0)
    rows_needed = nh + 1 + small.shape[0]
    unit = 8 << row_steps
    rows_total = -(-rows_needed // unit) * unit
    left = jnp.concatenate(
        [
            hidden_one,
            jnp.ones((1, ncells), hidden_one.dtype),
            jnp.zeros((rows_total - nh - 1, ncells), hidden_one.dtype),
        ],
        0,
    )
    packed = jnp.einsum("gc,hc->gh", left, delta_two, preferred_element_type=jnp.float32)
    packed = lax.dynamic_update_slice(packed, small, (nh + 1, 0))
    windows = {
        1: (particle_work, (feats_bar, recv_cell, slot, live, rate, slip)),
        2: (velocity_work, (feats_bar,)),
    }
    packed, results = tree_allreduce(packed, nz, ny, windows)
    slip_bar, rate_bar = results[1]
    velocity_bar = results[2]
    grad_w_mid = packed[:nh]
    grad_b_mid = packed[nh]
    grad_w_in = packed[nh + 1 : nh + 1 + grad_w_in.shape[0]]
    start = nh + 1 + grad_w_in.shape[0]
    grad_b_in = packed[start]
    grad_w_out = packed[start + 1 : start + 1 + grad_w_out_t.shape[0]].T
    return (
        stress.reshape(stress.shape[0], ncz, ncy, ncx),
        velocity_bar,
        slip_bar,
        rate_bar,
        grad_w_in,
        grad_b_in,
        grad_w_mid,
        grad_b_mid,
        grad_w_out,
    )


def solution(mesh):
    return jax.shard_map(
        shards,
        mesh=mesh,
        in_specs=(
            P(None, "gz", "gy", None),
            P(None, ("gz", "gy")),
            P(("gz", "gy")),
            P(("gz", "gy"), None),
            P(("gz", "gy")),
            P(("gz", "gy")),
            P(),
            P(),
            P(),
            P(),
            P(),
            P(None, "gz", "gy", None),
        ),
        out_specs=(
            P(None, "gz", "gy", None),
            P(None, "gz", "gy", None),
            P(None, ("gz", "gy")),
            P(("gz", "gy")),
            P(),
            P(),
            P(),
            P(),
            P(),
        ),
        check_vma=False,
    )
```

```python
import jax
import jax.numpy as jnp
from jax import lax
from jax.sharding import PartitionSpec as P


def with_halo(cells, sides, width):
    for axis, dim in sides:
        count = lax.axis_size(axis)
        head = lax.slice_in_dim(cells, 0, width, axis=dim)
        tail = lax.slice_in_dim(cells, cells.shape[dim] - width, cells.shape[dim], axis=dim)
        cells = jnp.concatenate(
            [
                lax.ppermute(tail, axis, [(i, (i + 1) % count) for i in range(count)]),
                cells,
                lax.ppermute(head, axis, [((i + 1) % count, i) for i in range(count)]),
            ],
            axis=dim,
        )
    return cells


def dsilu(value):
    sig = jax.nn.sigmoid(value)
    return sig * (1.0 + value * (1.0 - sig))


def deposit(forces, cell_row, ncells):
    block = min(512, ncells)
    count_blocks = ncells // block

    def deposit_one_block(index):
        start = index * block
        onehot = (
            cell_row[0][:, None] == start + jnp.arange(block, dtype=jnp.int32)[None, :]
        ).astype(jnp.float32)
        return jnp.dot(
            forces, onehot, precision=lax.Precision.HIGHEST, preferred_element_type=jnp.float32
        )

    pieces = lax.map(deposit_one_block, jnp.arange(count_blocks, dtype=jnp.int32))
    return pieces.transpose(1, 0, 2).reshape(forces.shape[0], ncells)


def collect(values, cell_row, ncells):
    block = min(512, ncells)
    count_blocks = ncells // block

    def collect_one_block(index, total):
        start = index * block
        onehot = (
            start + jnp.arange(block, dtype=jnp.int32)[:, None] == cell_row[0][None, :]
        ).astype(jnp.float32)
        return total + jnp.dot(
            values, onehot, precision=lax.Precision.HIGHEST, preferred_element_type=jnp.float32
        )

    init = jnp.zeros((values.shape[0], cell_row.shape[1]), jnp.float32)
    return lax.fori_loop(0, count_blocks, collect_one_block, init)


def tree_dims(nz, ny):
    gy_bits = [("gy", b) for b in range((ny - 1).bit_length())]
    gz_bits = [("gz", b) for b in range((nz - 1).bit_length())]
    dims = gy_bits + gz_bits
    if len(gy_bits) < 2 or not gz_bits:
        return lambda index: dims
    first, second = [gy_bits[0], gy_bits[1], gz_bits[0]], [gy_bits[0], gz_bits[0], gy_bits[1]]
    rest = gy_bits[2:] + gz_bits[1:]
    return lambda index: (first if index % ny % 2 == 0 else second) + rest


def tree_allreduce(packed, nz, ny, windows, first_step):
    orders = tree_dims(nz, ny)
    count = nz * ny
    steps = len(orders(0))
    lane_steps = min(steps, 3)

    def bit(index, dim):
        row, col = divmod(index, ny)
        return ((row if dim[0] == "gz" else col) >> dim[1]) & 1

    def partner(index, dim):
        row, col = divmod(index, ny)
        if dim[0] == "gz":
            row ^= 1 << dim[1]
        else:
            col ^= 1 << dim[1]
        return row * ny + col

    me = lax.axis_index("gz") * ny + lax.axis_index("gy")
    table = jnp.array([[bit(i, orders(i)[k]) for k in range(steps)] for i in range(count)], jnp.int32)
    mine = table[me]
    pairs = [[(i, partner(i, orders(i)[k])) for i in range(count)] for k in range(steps)]
    results = {}

    def exchange(send, k, key):
        if key not in windows:
            return lax.ppermute(send, ("gz", "gy"), pairs[k])
        work, inputs = windows[key]
        send, inputs = lax.optimization_barrier((send, inputs))
        got = lax.ppermute(send, ("gz", "gy"), pairs[k])
        outputs = work(*inputs)
        got, results[key] = lax.optimization_barrier((got, outputs))
        return got

    for k in range(steps):
        axis = 1 if k < lane_steps else 0
        if k == 0:
            keep, send = first_step(mine[0])
        else:
            half = packed.shape[axis] // 2
            keep = lax.dynamic_slice_in_dim(packed, mine[k] * half, half, axis)
            send = lax.dynamic_slice_in_dim(packed, (1 - mine[k]) * half, half, axis)
        packed = keep + exchange(send, k, k)
    for k in reversed(range(1, steps)):
        axis = 1 if k < lane_steps else 0
        got = exchange(packed, k, steps + k)
        low = mine[k] == 0
        packed = jnp.concatenate(
            [jnp.where(low, packed, got), jnp.where(low, got, packed)], axis
        )
    got = exchange(packed, 0, steps)
    low = mine[0] == 0
    return (jnp.where(low, packed, got), jnp.where(low, got, packed)), results


def roll_diff(field):
    return (jnp.roll(field, -1, 3) - jnp.roll(field, 1, 3)) * 0.5


def shards(velocity, slip, rate, owner, cell, count, w_in, b_in, w_mid, b_mid, w_out, tau_bar):
    nparts = slip.shape[1]
    slabs = lax.axis_size("gz")
    capacity = 2 * nparts // slabs
    width_all = slabs * capacity
    ncz, ncy, ncx = (velocity.shape[1], velocity.shape[2], velocity.shape[3])
    ncells = ncz * ncy * ncx
    padded = with_halo(velocity, (("gz", 1), ("gy", 2)), 1)
    core = padded[:, 1:-1, 1:-1]
    along_z = (padded[:, 2:, 1:-1] - padded[:, :-2, 1:-1]) * 0.5
    along_y = (padded[:, 1:-1, 2:] - padded[:, 1:-1, :-2]) * 0.5
    grads = jnp.stack([along_z, along_y, roll_diff(core)], 1).reshape(9, ncells)
    live = jnp.arange(nparts, dtype=jnp.int32) < count[0]
    force = jnp.where(live[None, :], rate[None, :] * slip, 0.0)
    owners = owner[:, 0]
    member = (owners[:, None] == jnp.arange(slabs, dtype=jnp.int32)[None, :]).astype(jnp.int32)
    before = jnp.cumsum(member, 0) - member
    position = jnp.sum(before * member, 1)
    slot = owners * capacity + position
    payload = jnp.concatenate(
        [force, jnp.where(live, cell, -1).astype(jnp.float32)[None]], 0
    )
    base = jnp.concatenate(
        [jnp.zeros((3, width_all), jnp.float32), jnp.full((1, width_all), -1.0, jnp.float32)], 0
    )
    received = lax.all_to_all(
        base.at[:, slot].set(payload), "gz", split_axis=1, concat_axis=1, tiled=True
    )
    recv_force = received[:3]
    recv_cell = received[3:].astype(jnp.int32)
    source = deposit(recv_force, recv_cell, ncells)
    feats = jnp.concatenate([grads, source], 0).astype(jnp.bfloat16)
    tbar = tau_bar.reshape(tau_bar.shape[0], ncells)
    pre1 = jnp.einsum("fh,fc->hc", w_in, feats, preferred_element_type=jnp.float32) + b_in[:, None]
    hidden_one = jax.nn.silu(pre1).astype(jnp.bfloat16)
    pre2 = (
        jnp.einsum("gh,gc->hc", w_mid, hidden_one, preferred_element_type=jnp.float32)
        + b_mid[:, None]
    )
    hidden_two = jax.nn.silu(pre2).astype(jnp.bfloat16)
    stress = jnp.einsum("ho,hc->oc", w_out, hidden_two, preferred_element_type=jnp.float32)
    grad_w_out_t = jnp.einsum("oc,hc->oh", tbar, hidden_two, preferred_element_type=jnp.float32)
    back_two = jnp.einsum("ho,oc->hc", w_out, tbar, preferred_element_type=jnp.float32)
    delta_two = (back_two * dsilu(pre2)).astype(jnp.bfloat16)
    back_one = jnp.einsum("gh,hc->gc", w_mid, delta_two, preferred_element_type=jnp.float32)
    delta_one = (back_one * dsilu(pre1)).astype(jnp.bfloat16)
    grad_w_in = jnp.einsum("fc,hc->fh", feats, delta_one, preferred_element_type=jnp.float32)
    grad_b_in = jnp.sum(delta_one.astype(jnp.float32), 1)
    nz, ny = lax.axis_size("gz"), lax.axis_size("gy")
    count = nz * ny
    feats_bar = jnp.einsum("fh,hc->fc", w_in, delta_one, preferred_element_type=jnp.float32)

    def velocity_work(feats_bar):
        grads_bar = feats_bar[:9].reshape(3, 3, ncz, ncy, ncx)
        zpad = with_halo(grads_bar[:, 0], (("gz", 1),), 1)
        ypad = with_halo(grads_bar[:, 1], (("gy", 2),), 1)
        term_z = (zpad[:, 2:] - zpad[:, :-2]) * 0.5
        term_y = (ypad[:, :, 2:] - ypad[:, :, :-2]) * 0.5
        term_x = roll_diff(grads_bar[:, 2])
        return -(term_z + term_y + term_x)

    def particle_work(feats_bar, recv_cell, slot, live, rate, slip):
        per_slot = collect(feats_bar[9:12], recv_cell, ncells)
        returned = lax.all_to_all(per_slot, "gz", split_axis=1, concat_axis=1, tiled=True)
        at_particle = returned[:, slot]
        slip_bar = jnp.where(live[None, :], rate[None, :] * at_particle, 0.0)
        rate_bar = jnp.where(live, jnp.sum(slip * at_particle, 0), 0.0)
        return slip_bar, rate_bar

    steps = (count - 1).bit_length()
    row_steps = max(steps - 3, 0)
    nh = hidden_one.shape[0]
    small = jnp.concatenate([grad_w_in, grad_b_in[None], grad_w_out_t], 0)
    rows_needed = nh + 1 + small.shape[0]
    unit = 8 << row_steps
    rows_total = -(-rows_needed // unit) * unit
    left = jnp.concatenate(
        [
            hidden_one,
            jnp.ones((1, ncells), hidden_one.dtype),
            jnp.zeros((rows_total - nh - 1, ncells), hidden_one.dtype),
        ],
        0,
    )
    half = delta_two.shape[0] // 2

    def first_step(low_bit):
        def part(offset):
            right = lax.dynamic_slice_in_dim(delta_two, offset, half, 0)
            out = jnp.einsum("gc,hc->gh", left, right, preferred_element_type=jnp.float32)
            return lax.dynamic_update_slice(
                out, lax.dynamic_slice_in_dim(small, offset, half, 1), (nh + 1, 0)
            )

        return part(low_bit * half), part((1 - low_bit) * half)

    windows = {
        1: (particle_work, (feats_bar, recv_cell, slot, live, rate, slip)),
        2: (velocity_work, (feats_bar,)),
    }
    (low_part, high_part), results = tree_allreduce(None, nz, ny, windows, first_step)
    packed = jnp.concatenate([low_part, high_part], 1)
    slip_bar, rate_bar = results[1]
    velocity_bar = results[2]
    grad_w_mid = packed[:nh]
    grad_b_mid = packed[nh]
    grad_w_in = packed[nh + 1 : nh + 1 + grad_w_in.shape[0]]
    start = nh + 1 + grad_w_in.shape[0]
    grad_b_in = packed[start]
    grad_w_out = packed[start + 1 : start + 1 + grad_w_out_t.shape[0]].T
    return (
        stress.reshape(stress.shape[0], ncz, ncy, ncx),
        velocity_bar,
        slip_bar,
        rate_bar,
        grad_w_in,
        grad_b_in,
        grad_w_mid,
        grad_b_mid,
        grad_w_out,
    )


def solution(mesh):
    return jax.shard_map(
        shards,
        mesh=mesh,
        in_specs=(
            P(None, "gz", "gy", None),
            P(None, ("gz", "gy")),
            P(("gz", "gy")),
            P(("gz", "gy"), None),
            P(("gz", "gy")),
            P(("gz", "gy")),
            P(),
            P(),
            P(),
            P(),
            P(),
            P(None, "gz", "gy", None),
        ),
        out_specs=(
            P(None, "gz", "gy", None),
            P(None, "gz", "gy", None),
            P(None, ("gz", "gy")),
            P(("gz", "gy")),
            P(),
            P(),
            P(),
            P(),
            P(),
        ),
        check_vma=False,
    )
```

```python
import jax
import jax.numpy as jnp
from jax import lax
from jax.sharding import PartitionSpec as P


def with_halo(cells, sides, width):
    for axis, dim in sides:
        count = lax.axis_size(axis)
        head = lax.slice_in_dim(cells, 0, width, axis=dim)
        tail = lax.slice_in_dim(cells, cells.shape[dim] - width, cells.shape[dim], axis=dim)
        cells = jnp.concatenate(
            [
                lax.ppermute(tail, axis, [(i, (i + 1) % count) for i in range(count)]),
                cells,
                lax.ppermute(head, axis, [((i + 1) % count, i) for i in range(count)]),
            ],
            axis=dim,
        )
    return cells


def dsilu(value):
    sig = jax.nn.sigmoid(value)
    return sig * (1.0 + value * (1.0 - sig))


def deposit(forces, cell_row, ncells):
    block = min(512, ncells)
    count_blocks = ncells // block

    def deposit_one_block(index):
        start = index * block
        onehot = (
            cell_row[0][:, None] == start + jnp.arange(block, dtype=jnp.int32)[None, :]
        ).astype(jnp.float32)
        return jnp.dot(
            forces, onehot, precision=lax.Precision.HIGHEST, preferred_element_type=jnp.float32
        )

    pieces = lax.map(deposit_one_block, jnp.arange(count_blocks, dtype=jnp.int32))
    return pieces.transpose(1, 0, 2).reshape(forces.shape[0], ncells)


def collect(values, cell_row, ncells):
    block = min(512, ncells)
    count_blocks = ncells // block

    def collect_one_block(index, total):
        start = index * block
        onehot = (
            start + jnp.arange(block, dtype=jnp.int32)[:, None] == cell_row[0][None, :]
        ).astype(jnp.float32)
        return total + jnp.dot(
            values, onehot, precision=lax.Precision.HIGHEST, preferred_element_type=jnp.float32
        )

    init = jnp.zeros((values.shape[0], cell_row.shape[1]), jnp.float32)
    return lax.fori_loop(0, count_blocks, collect_one_block, init)


def tree_dims(nz, ny):
    gy_bits = [("gy", b) for b in range((ny - 1).bit_length())]
    gz_bits = [("gz", b) for b in range((nz - 1).bit_length())]
    dims = gy_bits + gz_bits
    if len(gy_bits) < 2 or not gz_bits:
        return lambda index: dims
    first, second = [gy_bits[0], gy_bits[1], gz_bits[0]], [gy_bits[0], gz_bits[0], gy_bits[1]]
    rest = gy_bits[2:] + gz_bits[1:]
    return lambda index: (first if index % ny % 2 == 0 else second) + rest


def tree_allreduce(packed, nz, ny, windows, first_step):
    orders = tree_dims(nz, ny)
    count = nz * ny
    steps = len(orders(0))
    lane_steps = min(steps, 3)

    def bit(index, dim):
        row, col = divmod(index, ny)
        return ((row if dim[0] == "gz" else col) >> dim[1]) & 1

    def partner(index, dim):
        row, col = divmod(index, ny)
        if dim[0] == "gz":
            row ^= 1 << dim[1]
        else:
            col ^= 1 << dim[1]
        return row * ny + col

    me = lax.axis_index("gz") * ny + lax.axis_index("gy")
    table = jnp.array([[bit(i, orders(i)[k]) for k in range(steps)] for i in range(count)], jnp.int32)
    mine = table[me]
    pairs = [[(i, partner(i, orders(i)[k])) for i in range(count)] for k in range(steps)]
    results = {}

    def exchange(send, k, key):
        if key not in windows:
            return lax.ppermute(send, ("gz", "gy"), pairs[k])
        work, inputs = windows[key]
        send, inputs = lax.optimization_barrier((send, inputs))
        got = lax.ppermute(send, ("gz", "gy"), pairs[k])
        outputs = work(*inputs)
        got, results[key] = lax.optimization_barrier((got, outputs))
        return got

    halving = max(steps - 1, 1)
    for k in range(halving):
        axis = 1 if k < lane_steps else 0
        if k == 0:
            keep, send = first_step(mine[0])
        else:
            half = packed.shape[axis] // 2
            keep = lax.dynamic_slice_in_dim(packed, mine[k] * half, half, axis)
            send = lax.dynamic_slice_in_dim(packed, (1 - mine[k]) * half, half, axis)
        packed = keep + exchange(send, k, k)
    for k in range(halving, steps):
        packed = packed + exchange(packed, k, k)
    for k in reversed(range(1, halving)):
        axis = 1 if k < lane_steps else 0
        got = exchange(packed, k, steps + k)
        low = mine[k] == 0
        packed = jnp.concatenate(
            [jnp.where(low, packed, got), jnp.where(low, got, packed)], axis
        )
    got = exchange(packed, 0, steps)
    low = mine[0] == 0
    return (jnp.where(low, packed, got), jnp.where(low, got, packed)), results


def roll_diff(field):
    return (jnp.roll(field, -1, 3) - jnp.roll(field, 1, 3)) * 0.5


def shards(velocity, slip, rate, owner, cell, count, w_in, b_in, w_mid, b_mid, w_out, tau_bar):
    nparts = slip.shape[1]
    slabs = lax.axis_size("gz")
    capacity = 2 * nparts // slabs
    width_all = slabs * capacity
    ncz, ncy, ncx = (velocity.shape[1], velocity.shape[2], velocity.shape[3])
    ncells = ncz * ncy * ncx
    padded = with_halo(velocity, (("gz", 1), ("gy", 2)), 1)
    core = padded[:, 1:-1, 1:-1]
    along_z = (padded[:, 2:, 1:-1] - padded[:, :-2, 1:-1]) * 0.5
    along_y = (padded[:, 1:-1, 2:] - padded[:, 1:-1, :-2]) * 0.5
    grads = jnp.stack([along_z, along_y, roll_diff(core)], 1).reshape(9, ncells)
    live = jnp.arange(nparts, dtype=jnp.int32) < count[0]
    force = jnp.where(live[None, :], rate[None, :] * slip, 0.0)
    owners = owner[:, 0]
    member = (owners[:, None] == jnp.arange(slabs, dtype=jnp.int32)[None, :]).astype(jnp.int32)
    before = jnp.cumsum(member, 0) - member
    position = jnp.sum(before * member, 1)
    slot = owners * capacity + position
    payload = jnp.concatenate(
        [force, jnp.where(live, cell, -1).astype(jnp.float32)[None]], 0
    )
    base = jnp.concatenate(
        [jnp.zeros((3, width_all), jnp.float32), jnp.full((1, width_all), -1.0, jnp.float32)], 0
    )
    received = lax.all_to_all(
        base.at[:, slot].set(payload), "gz", split_axis=1, concat_axis=1, tiled=True
    )
    recv_force = received[:3]
    recv_cell = received[3:].astype(jnp.int32)
    source = deposit(recv_force, recv_cell, ncells)
    feats = jnp.concatenate([grads, source], 0).astype(jnp.bfloat16)
    tbar = tau_bar.reshape(tau_bar.shape[0], ncells)
    pre1 = jnp.einsum("fh,fc->hc", w_in, feats, preferred_element_type=jnp.float32) + b_in[:, None]
    hidden_one = jax.nn.silu(pre1).astype(jnp.bfloat16)
    pre2 = (
        jnp.einsum("gh,gc->hc", w_mid, hidden_one, preferred_element_type=jnp.float32)
        + b_mid[:, None]
    )
    hidden_two = jax.nn.silu(pre2).astype(jnp.bfloat16)
    stress = jnp.einsum("ho,hc->oc", w_out, hidden_two, preferred_element_type=jnp.float32)
    grad_w_out_t = jnp.einsum("oc,hc->oh", tbar, hidden_two, preferred_element_type=jnp.float32)
    back_two = jnp.einsum("ho,oc->hc", w_out, tbar, preferred_element_type=jnp.float32)
    delta_two = (back_two * dsilu(pre2)).astype(jnp.bfloat16)
    back_one = jnp.einsum("gh,hc->gc", w_mid, delta_two, preferred_element_type=jnp.float32)
    delta_one = (back_one * dsilu(pre1)).astype(jnp.bfloat16)
    grad_w_in = jnp.einsum("fc,hc->fh", feats, delta_one, preferred_element_type=jnp.float32)
    grad_b_in = jnp.sum(delta_one.astype(jnp.float32), 1)
    nz, ny = lax.axis_size("gz"), lax.axis_size("gy")
    count = nz * ny
    feats_bar = jnp.einsum("fh,hc->fc", w_in, delta_one, preferred_element_type=jnp.float32)

    def velocity_work(feats_bar):
        grads_bar = feats_bar[:9].reshape(3, 3, ncz, ncy, ncx)
        zpad = with_halo(grads_bar[:, 0], (("gz", 1),), 1)
        ypad = with_halo(grads_bar[:, 1], (("gy", 2),), 1)
        term_z = (zpad[:, 2:] - zpad[:, :-2]) * 0.5
        term_y = (ypad[:, :, 2:] - ypad[:, :, :-2]) * 0.5
        term_x = roll_diff(grads_bar[:, 2])
        return -(term_z + term_y + term_x)

    def particle_work(feats_bar, recv_cell, slot, live, rate, slip):
        per_slot = collect(feats_bar[9:12], recv_cell, ncells)
        returned = lax.all_to_all(per_slot, "gz", split_axis=1, concat_axis=1, tiled=True)
        at_particle = returned[:, slot]
        slip_bar = jnp.where(live[None, :], rate[None, :] * at_particle, 0.0)
        rate_bar = jnp.where(live, jnp.sum(slip * at_particle, 0), 0.0)
        return slip_bar, rate_bar

    steps = (count - 1).bit_length()
    row_steps = max(steps - 3, 0)
    nh = hidden_one.shape[0]
    small = jnp.concatenate([grad_w_in, grad_b_in[None], grad_w_out_t], 0)
    rows_needed = nh + 1 + small.shape[0]
    unit = 8 << row_steps
    rows_total = -(-rows_needed // unit) * unit
    left = jnp.concatenate(
        [
            hidden_one,
            jnp.ones((1, ncells), hidden_one.dtype),
            jnp.zeros((rows_total - nh - 1, ncells), hidden_one.dtype),
        ],
        0,
    )
    half = delta_two.shape[0] // 2

    def first_step(low_bit):
        def part(offset):
            right = lax.dynamic_slice_in_dim(delta_two, offset, half, 0)
            out = jnp.einsum("gc,hc->gh", left, right, preferred_element_type=jnp.float32)
            return lax.dynamic_update_slice(
                out, lax.dynamic_slice_in_dim(small, offset, half, 1), (nh + 1, 0)
            )

        return part(low_bit * half), part((1 - low_bit) * half)

    windows = {
        1: (particle_work, (feats_bar, recv_cell, slot, live, rate, slip)),
        2: (velocity_work, (feats_bar,)),
    }
    (low_part, high_part), results = tree_allreduce(None, nz, ny, windows, first_step)
    packed = jnp.concatenate([low_part, high_part], 1)
    slip_bar, rate_bar = results[1]
    velocity_bar = results[2]
    grad_w_mid = packed[:nh]
    grad_b_mid = packed[nh]
    grad_w_in = packed[nh + 1 : nh + 1 + grad_w_in.shape[0]]
    start = nh + 1 + grad_w_in.shape[0]
    grad_b_in = packed[start]
    grad_w_out = packed[start + 1 : start + 1 + grad_w_out_t.shape[0]].T
    return (
        stress.reshape(stress.shape[0], ncz, ncy, ncx),
        velocity_bar,
        slip_bar,
        rate_bar,
        grad_w_in,
        grad_b_in,
        grad_w_mid,
        grad_b_mid,
        grad_w_out,
    )


def solution(mesh):
    return jax.shard_map(
        shards,
        mesh=mesh,
        in_specs=(
            P(None, "gz", "gy", None),
            P(None, ("gz", "gy")),
            P(("gz", "gy")),
            P(("gz", "gy"), None),
            P(("gz", "gy")),
            P(("gz", "gy")),
            P(),
            P(),
            P(),
            P(),
            P(),
            P(None, "gz", "gy", None),
        ),
        out_specs=(
            P(None, "gz", "gy", None),
            P(None, "gz", "gy", None),
            P(None, ("gz", "gy")),
            P(("gz", "gy")),
            P(),
            P(),
            P(),
            P(),
            P(),
        ),
        check_vma=False,
    )
```

```python
import jax
import jax.numpy as jnp
from jax import lax
from jax.sharding import PartitionSpec as P


def with_halo(cells, sides, width):
    for axis, dim in sides:
        count = lax.axis_size(axis)
        head = lax.slice_in_dim(cells, 0, width, axis=dim)
        tail = lax.slice_in_dim(cells, cells.shape[dim] - width, cells.shape[dim], axis=dim)
        cells = jnp.concatenate(
            [
                lax.ppermute(tail, axis, [(i, (i + 1) % count) for i in range(count)]),
                cells,
                lax.ppermute(head, axis, [((i + 1) % count, i) for i in range(count)]),
            ],
            axis=dim,
        )
    return cells


def dsilu(value):
    sig = jax.nn.sigmoid(value)
    return sig * (1.0 + value * (1.0 - sig))


def deposit(forces, cell_row, ncells):
    block = min(512, ncells)
    count_blocks = ncells // block

    def deposit_one_block(index):
        start = index * block
        onehot = (
            cell_row[0][:, None] == start + jnp.arange(block, dtype=jnp.int32)[None, :]
        ).astype(jnp.float32)
        return jnp.dot(
            forces, onehot, precision=lax.Precision.HIGHEST, preferred_element_type=jnp.float32
        )

    pieces = lax.map(deposit_one_block, jnp.arange(count_blocks, dtype=jnp.int32))
    return pieces.transpose(1, 0, 2).reshape(forces.shape[0], ncells)


def collect(values, cell_row, ncells):
    block = min(512, ncells)
    count_blocks = ncells // block

    def collect_one_block(index, total):
        start = index * block
        onehot = (
            start + jnp.arange(block, dtype=jnp.int32)[:, None] == cell_row[0][None, :]
        ).astype(jnp.float32)
        return total + jnp.dot(
            values, onehot, precision=lax.Precision.HIGHEST, preferred_element_type=jnp.float32
        )

    init = jnp.zeros((values.shape[0], cell_row.shape[1]), jnp.float32)
    return lax.fori_loop(0, count_blocks, collect_one_block, init)


def tree_dims(nz, ny):
    gy_bits = [("gy", b) for b in range((ny - 1).bit_length())]
    gz_bits = [("gz", b) for b in range((nz - 1).bit_length())]
    dims = gy_bits + gz_bits
    if len(gy_bits) < 2 or not gz_bits:
        return lambda index: dims
    if len(gz_bits) < 2:
        first, second = [gy_bits[0], gy_bits[1], gz_bits[0]], [gy_bits[0], gz_bits[0], gy_bits[1]]
        rest = gy_bits[2:] + gz_bits[1:]
    else:
        first = [gy_bits[0], gy_bits[1], gz_bits[1], gz_bits[0]]
        second = [gy_bits[0], gz_bits[1], gz_bits[0], gy_bits[1]]
        rest = gy_bits[2:] + gz_bits[2:]
    return lambda index: (first if index % ny % 2 == 0 else second) + rest


def tree_allreduce(packed, nz, ny, windows, first_step):
    orders = tree_dims(nz, ny)
    count = nz * ny
    steps = len(orders(0))
    lane_steps = min(steps, 3)

    def bit(index, dim):
        row, col = divmod(index, ny)
        return ((row if dim[0] == "gz" else col) >> dim[1]) & 1

    def partner(index, dim):
        row, col = divmod(index, ny)
        if dim[0] == "gz":
            row ^= 1 << dim[1]
        else:
            col ^= 1 << dim[1]
        return row * ny + col

    me = lax.axis_index("gz") * ny + lax.axis_index("gy")
    table = jnp.array([[bit(i, orders(i)[k]) for k in range(steps)] for i in range(count)], jnp.int32)
    mine = table[me]
    pairs = [[(i, partner(i, orders(i)[k])) for i in range(count)] for k in range(steps)]
    results = {}

    def exchange(send, k, key):
        if key not in windows:
            return lax.ppermute(send, ("gz", "gy"), pairs[k])
        work, inputs = windows[key]
        send, inputs = lax.optimization_barrier((send, inputs))
        got = lax.ppermute(send, ("gz", "gy"), pairs[k])
        outputs = work(*inputs)
        got, results[key] = lax.optimization_barrier((got, outputs))
        return got

    halving = max(steps - 1, 1)
    for k in range(halving):
        axis = 1 if k < lane_steps else 0
        if k == 0:
            keep, send = first_step(mine[0])
        else:
            half = packed.shape[axis] // 2
            keep = lax.dynamic_slice_in_dim(packed, mine[k] * half, half, axis)
            send = lax.dynamic_slice_in_dim(packed, (1 - mine[k]) * half, half, axis)
        packed = keep + exchange(send, k, k)
    for k in range(halving, steps):
        packed = packed + exchange(packed, k, k)
    for k in reversed(range(1, halving)):
        axis = 1 if k < lane_steps else 0
        got = exchange(packed, k, steps + k)
        low = mine[k] == 0
        packed = jnp.concatenate(
            [jnp.where(low, packed, got), jnp.where(low, got, packed)], axis
        )
    got = exchange(packed, 0, steps)
    low = mine[0] == 0
    return (jnp.where(low, packed, got), jnp.where(low, got, packed)), results


def roll_diff(field):
    return (jnp.roll(field, -1, 3) - jnp.roll(field, 1, 3)) * 0.5


def shards(velocity, slip, rate, owner, cell, count, w_in, b_in, w_mid, b_mid, w_out, tau_bar):
    nparts = slip.shape[1]
    slabs = lax.axis_size("gz")
    capacity = 2 * nparts // slabs
    width_all = slabs * capacity
    ncz, ncy, ncx = (velocity.shape[1], velocity.shape[2], velocity.shape[3])
    ncells = ncz * ncy * ncx
    padded = with_halo(velocity, (("gz", 1), ("gy", 2)), 1)
    core = padded[:, 1:-1, 1:-1]
    along_z = (padded[:, 2:, 1:-1] - padded[:, :-2, 1:-1]) * 0.5
    along_y = (padded[:, 1:-1, 2:] - padded[:, 1:-1, :-2]) * 0.5
    grads = jnp.stack([along_z, along_y, roll_diff(core)], 1).reshape(9, ncells)
    live = jnp.arange(nparts, dtype=jnp.int32) < count[0]
    force = jnp.where(live[None, :], rate[None, :] * slip, 0.0)
    owners = owner[:, 0]
    member = (owners[:, None] == jnp.arange(slabs, dtype=jnp.int32)[None, :]).astype(jnp.int32)
    before = jnp.cumsum(member, 0) - member
    position = jnp.sum(before * member, 1)
    slot = owners * capacity + position
    payload = jnp.concatenate(
        [force, jnp.where(live, cell, -1).astype(jnp.float32)[None]], 0
    )
    base = jnp.concatenate(
        [jnp.zeros((3, width_all), jnp.float32), jnp.full((1, width_all), -1.0, jnp.float32)], 0
    )
    received = lax.all_to_all(
        base.at[:, slot].set(payload), "gz", split_axis=1, concat_axis=1, tiled=True
    )
    recv_force = received[:3]
    recv_cell = received[3:].astype(jnp.int32)
    source = deposit(recv_force, recv_cell, ncells)
    feats = jnp.concatenate([grads, source], 0).astype(jnp.bfloat16)
    tbar = tau_bar.reshape(tau_bar.shape[0], ncells)
    pre1 = jnp.einsum("fh,fc->hc", w_in, feats, preferred_element_type=jnp.float32) + b_in[:, None]
    hidden_one = jax.nn.silu(pre1).astype(jnp.bfloat16)
    pre2 = (
        jnp.einsum("gh,gc->hc", w_mid, hidden_one, preferred_element_type=jnp.float32)
        + b_mid[:, None]
    )
    hidden_two = jax.nn.silu(pre2).astype(jnp.bfloat16)
    stress = jnp.einsum("ho,hc->oc", w_out, hidden_two, preferred_element_type=jnp.float32)
    grad_w_out_t = jnp.einsum("oc,hc->oh", tbar, hidden_two, preferred_element_type=jnp.float32)
    back_two = jnp.einsum("ho,oc->hc", w_out, tbar, preferred_element_type=jnp.float32)
    delta_two = (back_two * dsilu(pre2)).astype(jnp.bfloat16)
    back_one = jnp.einsum("gh,hc->gc", w_mid, delta_two, preferred_element_type=jnp.float32)
    delta_one = (back_one * dsilu(pre1)).astype(jnp.bfloat16)
    grad_w_in = jnp.einsum("fc,hc->fh", feats, delta_one, preferred_element_type=jnp.float32)
    grad_b_in = jnp.sum(delta_one.astype(jnp.float32), 1)
    nz, ny = lax.axis_size("gz"), lax.axis_size("gy")
    count = nz * ny
    feats_bar = jnp.einsum("fh,hc->fc", w_in, delta_one, preferred_element_type=jnp.float32)

    def velocity_work(feats_bar):
        grads_bar = feats_bar[:9].reshape(3, 3, ncz, ncy, ncx)
        zpad = with_halo(grads_bar[:, 0], (("gz", 1),), 1)
        ypad = with_halo(grads_bar[:, 1], (("gy", 2),), 1)
        term_z = (zpad[:, 2:] - zpad[:, :-2]) * 0.5
        term_y = (ypad[:, :, 2:] - ypad[:, :, :-2]) * 0.5
        term_x = roll_diff(grads_bar[:, 2])
        return -(term_z + term_y + term_x)

    def particle_work(feats_bar, recv_cell, slot, live, rate, slip):
        per_slot = collect(feats_bar[9:12], recv_cell, ncells)
        returned = lax.all_to_all(per_slot, "gz", split_axis=1, concat_axis=1, tiled=True)
        at_particle = returned[:, slot]
        slip_bar = jnp.where(live[None, :], rate[None, :] * at_particle, 0.0)
        rate_bar = jnp.where(live, jnp.sum(slip * at_particle, 0), 0.0)
        return slip_bar, rate_bar

    steps = (count - 1).bit_length()
    row_steps = max(steps - 3, 0)
    nh = hidden_one.shape[0]
    small = jnp.concatenate([grad_w_in, grad_b_in[None], grad_w_out_t], 0)
    rows_needed = nh + 1 + small.shape[0]
    unit = 8 << row_steps
    rows_total = -(-rows_needed // unit) * unit
    left = jnp.concatenate(
        [
            hidden_one,
            jnp.ones((1, ncells), hidden_one.dtype),
            jnp.zeros((rows_total - nh - 1, ncells), hidden_one.dtype),
        ],
        0,
    )
    half = delta_two.shape[0] // 2

    def first_step(low_bit):
        def part(offset):
            right = lax.dynamic_slice_in_dim(delta_two, offset, half, 0)
            out = jnp.einsum("gc,hc->gh", left, right, preferred_element_type=jnp.float32)
            return lax.dynamic_update_slice(
                out, lax.dynamic_slice_in_dim(small, offset, half, 1), (nh + 1, 0)
            )

        return part(low_bit * half), part((1 - low_bit) * half)

    windows = {
        1: (particle_work, (feats_bar, recv_cell, slot, live, rate, slip)),
        2: (velocity_work, (feats_bar,)),
    }
    (low_part, high_part), results = tree_allreduce(None, nz, ny, windows, first_step)
    packed = jnp.concatenate([low_part, high_part], 1)
    slip_bar, rate_bar = results[1]
    velocity_bar = results[2]
    grad_w_mid = packed[:nh]
    grad_b_mid = packed[nh]
    grad_w_in = packed[nh + 1 : nh + 1 + grad_w_in.shape[0]]
    start = nh + 1 + grad_w_in.shape[0]
    grad_b_in = packed[start]
    grad_w_out = packed[start + 1 : start + 1 + grad_w_out_t.shape[0]].T
    return (
        stress.reshape(stress.shape[0], ncz, ncy, ncx),
        velocity_bar,
        slip_bar,
        rate_bar,
        grad_w_in,
        grad_b_in,
        grad_w_mid,
        grad_b_mid,
        grad_w_out,
    )


def solution(mesh):
    return jax.shard_map(
        shards,
        mesh=mesh,
        in_specs=(
            P(None, "gz", "gy", None),
            P(None, ("gz", "gy")),
            P(("gz", "gy")),
            P(("gz", "gy"), None),
            P(("gz", "gy")),
            P(("gz", "gy")),
            P(),
            P(),
            P(),
            P(),
            P(),
            P(None, "gz", "gy", None),
        ),
        out_specs=(
            P(None, "gz", "gy", None),
            P(None, "gz", "gy", None),
            P(None, ("gz", "gy")),
            P(("gz", "gy")),
            P(),
            P(),
            P(),
            P(),
            P(),
        ),
        check_vma=False,
    )
```

```python
import jax
import jax.numpy as jnp
from jax import lax
from jax.sharding import PartitionSpec as P


def with_halo(cells, sides, width):
    for axis, dim in sides:
        count = lax.axis_size(axis)
        head = lax.slice_in_dim(cells, 0, width, axis=dim)
        tail = lax.slice_in_dim(cells, cells.shape[dim] - width, cells.shape[dim], axis=dim)
        cells = jnp.concatenate(
            [
                lax.ppermute(tail, axis, [(i, (i + 1) % count) for i in range(count)]),
                cells,
                lax.ppermute(head, axis, [((i + 1) % count, i) for i in range(count)]),
            ],
            axis=dim,
        )
    return cells


def dsilu(value):
    sig = jax.nn.sigmoid(value)
    return sig * (1.0 + value * (1.0 - sig))


def deposit(forces, cell_row, ncells):
    block = min(512, ncells)
    count_blocks = ncells // block

    def deposit_one_block(index):
        start = index * block
        onehot = (
            cell_row[0][:, None] == start + jnp.arange(block, dtype=jnp.int32)[None, :]
        ).astype(jnp.float32)
        return jnp.dot(
            forces, onehot, precision=lax.Precision.HIGHEST, preferred_element_type=jnp.float32
        )

    pieces = lax.map(deposit_one_block, jnp.arange(count_blocks, dtype=jnp.int32))
    return pieces.transpose(1, 0, 2).reshape(forces.shape[0], ncells)


def collect(values, cell_row, ncells):
    block = min(512, ncells)
    count_blocks = ncells // block

    def collect_one_block(index, total):
        start = index * block
        onehot = (
            start + jnp.arange(block, dtype=jnp.int32)[:, None] == cell_row[0][None, :]
        ).astype(jnp.float32)
        return total + jnp.dot(
            values, onehot, precision=lax.Precision.HIGHEST, preferred_element_type=jnp.float32
        )

    init = jnp.zeros((values.shape[0], cell_row.shape[1]), jnp.float32)
    return lax.fori_loop(0, count_blocks, collect_one_block, init)


def tree_dims(nz, ny):
    gy_bits = [("gy", b) for b in range((ny - 1).bit_length())]
    gz_bits = [("gz", b) for b in range((nz - 1).bit_length())]
    dims = gy_bits + gz_bits
    if len(gy_bits) < 2 or not gz_bits:
        return lambda index: dims
    if len(gz_bits) < 2:
        first, second = [gy_bits[0], gy_bits[1], gz_bits[0]], [gy_bits[0], gz_bits[0], gy_bits[1]]
        rest = gy_bits[2:] + gz_bits[1:]
    else:
        first = [gy_bits[0], gy_bits[1], gz_bits[1], gz_bits[0]]
        second = [gy_bits[0], gz_bits[1], gz_bits[0], gy_bits[1]]
        rest = gy_bits[2:] + gz_bits[2:]
    return lambda index: (first if index % ny % 2 == 0 else second) + rest


def tree_allreduce(packed, nz, ny, windows, first_step):
    orders = tree_dims(nz, ny)
    count = nz * ny
    steps = len(orders(0))
    lane_steps = min(steps, 3)

    def bit(index, dim):
        row, col = divmod(index, ny)
        return ((row if dim[0] == "gz" else col) >> dim[1]) & 1

    def partner(index, dim):
        row, col = divmod(index, ny)
        if dim[0] == "gz":
            row ^= 1 << dim[1]
        else:
            col ^= 1 << dim[1]
        return row * ny + col

    me = lax.axis_index("gz") * ny + lax.axis_index("gy")
    table = jnp.array([[bit(i, orders(i)[k]) for k in range(steps)] for i in range(count)], jnp.int32)
    mine = table[me]
    pairs = [[(i, partner(i, orders(i)[k])) for i in range(count)] for k in range(steps)]
    results = {}

    def exchange(send, k, key):
        if key not in windows:
            return lax.ppermute(send, ("gz", "gy"), pairs[k])
        work, inputs = windows[key]
        send, inputs = lax.optimization_barrier((send, inputs))
        got = lax.ppermute(send, ("gz", "gy"), pairs[k])
        outputs = work(*inputs)
        got, results[key] = lax.optimization_barrier((got, outputs))
        return got

    halving = max(steps - 1, 1)
    for k in range(halving):
        axis = 1 if k < lane_steps else 0
        if k == 0:
            keep, send = first_step(mine[0])
        else:
            half = packed.shape[axis] // 2
            keep = lax.dynamic_slice_in_dim(packed, mine[k] * half, half, axis)
            send = lax.dynamic_slice_in_dim(packed, (1 - mine[k]) * half, half, axis)
        packed = keep + exchange(send, k, k)
    for k in range(halving, steps):
        packed = packed + exchange(packed, k, k)
    for k in reversed(range(1, halving)):
        axis = 1 if k < lane_steps else 0
        got = exchange(packed, k, steps + k)
        low = mine[k] == 0
        packed = jnp.concatenate(
            [jnp.where(low, packed, got), jnp.where(low, got, packed)], axis
        )
    got = exchange(packed, 0, steps)
    return (packed, got, mine[0] == 0), results


def roll_diff(field):
    return (jnp.roll(field, -1, 3) - jnp.roll(field, 1, 3)) * 0.5


def shards(velocity, slip, rate, owner, cell, count, w_in, b_in, w_mid, b_mid, w_out, tau_bar):
    nparts = slip.shape[1]
    slabs = lax.axis_size("gz")
    capacity = 2 * nparts // slabs
    width_all = slabs * capacity
    ncz, ncy, ncx = (velocity.shape[1], velocity.shape[2], velocity.shape[3])
    ncells = ncz * ncy * ncx
    padded = with_halo(velocity, (("gz", 1), ("gy", 2)), 1)
    core = padded[:, 1:-1, 1:-1]
    along_z = (padded[:, 2:, 1:-1] - padded[:, :-2, 1:-1]) * 0.5
    along_y = (padded[:, 1:-1, 2:] - padded[:, 1:-1, :-2]) * 0.5
    grads = jnp.stack([along_z, along_y, roll_diff(core)], 1).reshape(9, ncells)
    live = jnp.arange(nparts, dtype=jnp.int32) < count[0]
    force = jnp.where(live[None, :], rate[None, :] * slip, 0.0)
    owners = owner[:, 0]
    member = (owners[:, None] == jnp.arange(slabs, dtype=jnp.int32)[None, :]).astype(jnp.int32)
    before = jnp.cumsum(member, 0) - member
    position = jnp.sum(before * member, 1)
    slot = owners * capacity + position
    payload = jnp.concatenate(
        [force, jnp.where(live, cell, -1).astype(jnp.float32)[None]], 0
    )
    base = jnp.concatenate(
        [jnp.zeros((3, width_all), jnp.float32), jnp.full((1, width_all), -1.0, jnp.float32)], 0
    )
    received = lax.all_to_all(
        base.at[:, slot].set(payload), "gz", split_axis=1, concat_axis=1, tiled=True
    )
    recv_force = received[:3]
    recv_cell = received[3:].astype(jnp.int32)
    source = deposit(recv_force, recv_cell, ncells)
    feats = jnp.concatenate([grads, source], 0).astype(jnp.bfloat16)
    tbar = tau_bar.reshape(tau_bar.shape[0], ncells)
    pre1 = jnp.einsum("fh,fc->hc", w_in, feats, preferred_element_type=jnp.float32) + b_in[:, None]
    hidden_one = jax.nn.silu(pre1).astype(jnp.bfloat16)
    pre2 = (
        jnp.einsum("gh,gc->hc", w_mid, hidden_one, preferred_element_type=jnp.float32)
        + b_mid[:, None]
    )
    hidden_two = jax.nn.silu(pre2).astype(jnp.bfloat16)
    stress = jnp.einsum("ho,hc->oc", w_out, hidden_two, preferred_element_type=jnp.float32)
    grad_w_out_t = jnp.einsum("oc,hc->oh", tbar, hidden_two, preferred_element_type=jnp.float32)
    back_two = jnp.einsum("ho,oc->hc", w_out, tbar, preferred_element_type=jnp.float32)
    delta_two = (back_two * dsilu(pre2)).astype(jnp.bfloat16)
    back_one = jnp.einsum("gh,hc->gc", w_mid, delta_two, preferred_element_type=jnp.float32)
    delta_one = (back_one * dsilu(pre1)).astype(jnp.bfloat16)
    grad_w_in = jnp.einsum("fc,hc->fh", feats, delta_one, preferred_element_type=jnp.float32)
    grad_b_in = jnp.sum(delta_one.astype(jnp.float32), 1)
    nz, ny = lax.axis_size("gz"), lax.axis_size("gy")
    count = nz * ny
    feats_bar = jnp.einsum("fh,hc->fc", w_in, delta_one, preferred_element_type=jnp.float32)

    def velocity_work(feats_bar):
        grads_bar = feats_bar[:9].reshape(3, 3, ncz, ncy, ncx)
        zpad = with_halo(grads_bar[:, 0], (("gz", 1),), 1)
        ypad = with_halo(grads_bar[:, 1], (("gy", 2),), 1)
        term_z = (zpad[:, 2:] - zpad[:, :-2]) * 0.5
        term_y = (ypad[:, :, 2:] - ypad[:, :, :-2]) * 0.5
        term_x = roll_diff(grads_bar[:, 2])
        return -(term_z + term_y + term_x)

    def particle_work(feats_bar, recv_cell, slot, live, rate, slip):
        per_slot = collect(feats_bar[9:12], recv_cell, ncells)
        returned = lax.all_to_all(per_slot, "gz", split_axis=1, concat_axis=1, tiled=True)
        at_particle = returned[:, slot]
        slip_bar = jnp.where(live[None, :], rate[None, :] * at_particle, 0.0)
        rate_bar = jnp.where(live, jnp.sum(slip * at_particle, 0), 0.0)
        return slip_bar, rate_bar

    steps = (count - 1).bit_length()
    row_steps = max(steps - 3, 0)
    nh = hidden_one.shape[0]
    small = jnp.concatenate([grad_w_in, grad_b_in[None], grad_w_out_t], 0)
    rows_needed = nh + 1 + small.shape[0]
    unit = 8 << row_steps
    rows_total = -(-rows_needed // unit) * unit
    left = jnp.concatenate(
        [
            hidden_one,
            jnp.ones((1, ncells), hidden_one.dtype),
            jnp.zeros((rows_total - nh - 1, ncells), hidden_one.dtype),
        ],
        0,
    )
    half = delta_two.shape[0] // 2

    def first_step(low_bit):
        def part(offset):
            right = lax.dynamic_slice_in_dim(delta_two, offset, half, 0)
            out = jnp.einsum("gc,hc->gh", left, right, preferred_element_type=jnp.float32)
            return lax.dynamic_update_slice(
                out, lax.dynamic_slice_in_dim(small, offset, half, 1), (nh + 1, 0)
            )

        return part(low_bit * half), part((1 - low_bit) * half)

    windows = {
        1: (particle_work, (feats_bar, recv_cell, slot, live, rate, slip)),
        2: (velocity_work, (feats_bar,)),
    }
    (own, got, low), results = tree_allreduce(None, nz, ny, windows, first_step)

    def rows(begin, end):
        a, b = own[begin:end], got[begin:end]
        return jnp.where(low, jnp.concatenate([a, b], 1), jnp.concatenate([b, a], 1))

    packed = rows(nh, rows_needed)
    slip_bar, rate_bar = results[1]
    velocity_bar = results[2]
    grad_w_mid = rows(0, nh)
    grad_b_mid = packed[0]
    grad_w_in = packed[1 : 1 + grad_w_in.shape[0]]
    start = 1 + grad_w_in.shape[0]
    grad_b_in = packed[start]
    grad_w_out = packed[start + 1 : start + 1 + grad_w_out_t.shape[0]].T
    return (
        stress.reshape(stress.shape[0], ncz, ncy, ncx),
        velocity_bar,
        slip_bar,
        rate_bar,
        grad_w_in,
        grad_b_in,
        grad_w_mid,
        grad_b_mid,
        grad_w_out,
    )


def solution(mesh):
    return jax.shard_map(
        shards,
        mesh=mesh,
        in_specs=(
            P(None, "gz", "gy", None),
            P(None, ("gz", "gy")),
            P(("gz", "gy")),
            P(("gz", "gy"), None),
            P(("gz", "gy")),
            P(("gz", "gy")),
            P(),
            P(),
            P(),
            P(),
            P(),
            P(None, "gz", "gy", None),
        ),
        out_specs=(
            P(None, "gz", "gy", None),
            P(None, "gz", "gy", None),
            P(None, ("gz", "gy")),
            P(("gz", "gy")),
            P(),
            P(),
            P(),
            P(),
            P(),
        ),
        check_vma=False,
    )
```

```python
import jax
import jax.numpy as jnp
from jax import lax
from jax.sharding import PartitionSpec as P


def with_halo(cells, sides, width):
    for axis, dim in sides:
        count = lax.axis_size(axis)
        head = lax.slice_in_dim(cells, 0, width, axis=dim)
        tail = lax.slice_in_dim(cells, cells.shape[dim] - width, cells.shape[dim], axis=dim)
        cells = jnp.concatenate(
            [
                lax.ppermute(tail, axis, [(i, (i + 1) % count) for i in range(count)]),
                cells,
                lax.ppermute(head, axis, [((i + 1) % count, i) for i in range(count)]),
            ],
            axis=dim,
        )
    return cells


def dsilu(value):
    sig = jax.nn.sigmoid(value)
    return sig * (1.0 + value * (1.0 - sig))


def deposit(forces, cell_row, ncells):
    block = min(512, ncells)
    count_blocks = ncells // block

    def deposit_one_block(index):
        start = index * block
        onehot = (
            cell_row[0][:, None] == start + jnp.arange(block, dtype=jnp.int32)[None, :]
        ).astype(jnp.float32)
        return jnp.dot(
            forces, onehot, precision=lax.Precision.HIGHEST, preferred_element_type=jnp.float32
        )

    pieces = lax.map(deposit_one_block, jnp.arange(count_blocks, dtype=jnp.int32))
    return pieces.transpose(1, 0, 2).reshape(forces.shape[0], ncells)


def collect(values, cell_row, ncells):
    block = min(512, ncells)
    count_blocks = ncells // block

    def collect_one_block(index, total):
        start = index * block
        onehot = (
            start + jnp.arange(block, dtype=jnp.int32)[:, None] == cell_row[0][None, :]
        ).astype(jnp.float32)
        return total + jnp.dot(
            values, onehot, precision=lax.Precision.HIGHEST, preferred_element_type=jnp.float32
        )

    init = jnp.zeros((values.shape[0], cell_row.shape[1]), jnp.float32)
    return lax.fori_loop(0, count_blocks, collect_one_block, init)


def tree_dims(nz, ny):
    gy_bits = [("gy", b) for b in range((ny - 1).bit_length())]
    gz_bits = [("gz", b) for b in range((nz - 1).bit_length())]
    dims = gy_bits + gz_bits
    if len(gy_bits) < 2 or not gz_bits:
        return lambda index: dims
    if len(gz_bits) < 2:
        first, second = [gy_bits[0], gy_bits[1], gz_bits[0]], [gy_bits[0], gz_bits[0], gy_bits[1]]
        rest = gy_bits[2:] + gz_bits[1:]
    else:
        first = [gy_bits[0], gy_bits[1], gz_bits[1], gz_bits[0]]
        second = [gy_bits[0], gz_bits[1], gz_bits[0], gy_bits[1]]
        rest = gy_bits[2:] + gz_bits[2:]
    return lambda index: (first if index % ny % 2 == 0 else second) + rest


def tree_allreduce(packed, nz, ny, windows, first_step):
    orders = tree_dims(nz, ny)
    count = nz * ny
    steps = len(orders(0))
    lane_steps = min(steps, 3)

    def bit(index, dim):
        row, col = divmod(index, ny)
        return ((row if dim[0] == "gz" else col) >> dim[1]) & 1

    def partner(index, dim):
        row, col = divmod(index, ny)
        if dim[0] == "gz":
            row ^= 1 << dim[1]
        else:
            col ^= 1 << dim[1]
        return row * ny + col

    me = lax.axis_index("gz") * ny + lax.axis_index("gy")
    table = jnp.array([[bit(i, orders(i)[k]) for k in range(steps)] for i in range(count)], jnp.int32)
    mine = table[me]
    pairs = [[(i, partner(i, orders(i)[k])) for i in range(count)] for k in range(steps)]
    results = {}

    def exchange(send, k, key):
        if key not in windows:
            return lax.ppermute(send, ("gz", "gy"), pairs[k])
        work, inputs = windows[key]
        send, inputs = lax.optimization_barrier((send, inputs))
        got = lax.ppermute(send, ("gz", "gy"), pairs[k])
        outputs = work(*inputs)
        got, results[key] = lax.optimization_barrier((got, outputs))
        return got

    halving = max(steps - 1, 1)
    for k in range(halving):
        axis = 1 if k < lane_steps else 0
        if k == 0:
            keep, send = first_step(mine[0])
        else:
            half = packed.shape[axis] // 2
            keep = lax.dynamic_slice_in_dim(packed, mine[k] * half, half, axis)
            send = lax.dynamic_slice_in_dim(packed, (1 - mine[k]) * half, half, axis)
        packed = keep + exchange(send, k, k)
    for k in range(halving, steps):
        packed = packed + exchange(packed, k, k)
    for k in reversed(range(1, halving)):
        axis = 1 if k < lane_steps else 0
        got = exchange(packed, k, steps + k)
        low = mine[k] == 0
        packed = jnp.concatenate(
            [jnp.where(low, packed, got), jnp.where(low, got, packed)], axis
        )
    got = exchange(packed, 0, steps)
    low = mine[0] == 0
    return (jnp.where(low, packed, got), jnp.where(low, got, packed)), results


def roll_diff(field):
    return (jnp.roll(field, -1, 3) - jnp.roll(field, 1, 3)) * 0.5


def shards(velocity, slip, rate, owner, cell, count, w_in, b_in, w_mid, b_mid, w_out, tau_bar):
    nparts = slip.shape[1]
    slabs = lax.axis_size("gz")
    capacity = 2 * nparts // slabs
    width_all = slabs * capacity
    ncz, ncy, ncx = (velocity.shape[1], velocity.shape[2], velocity.shape[3])
    ncells = ncz * ncy * ncx
    padded = with_halo(velocity, (("gz", 1), ("gy", 2)), 1)
    core = padded[:, 1:-1, 1:-1]
    along_z = (padded[:, 2:, 1:-1] - padded[:, :-2, 1:-1]) * 0.5
    along_y = (padded[:, 1:-1, 2:] - padded[:, 1:-1, :-2]) * 0.5
    grads = jnp.stack([along_z, along_y, roll_diff(core)], 1).reshape(9, ncells)
    live = jnp.arange(nparts, dtype=jnp.int32) < count[0]
    force = jnp.where(live[None, :], rate[None, :] * slip, 0.0)
    owners = owner[:, 0]
    member = (owners[:, None] == jnp.arange(slabs, dtype=jnp.int32)[None, :]).astype(jnp.int32)
    before = jnp.cumsum(member, 0) - member
    position = jnp.sum(before * member, 1)
    slot = owners * capacity + position
    payload = jnp.concatenate(
        [force, jnp.where(live, cell, -1).astype(jnp.float32)[None]], 0
    )
    base = jnp.concatenate(
        [jnp.zeros((3, width_all), jnp.float32), jnp.full((1, width_all), -1.0, jnp.float32)], 0
    )
    received = lax.all_to_all(
        base.at[:, slot].set(payload), "gz", split_axis=1, concat_axis=1, tiled=True
    )
    recv_force = received[:3]
    recv_cell = received[3:].astype(jnp.int32)
    source = deposit(recv_force, recv_cell, ncells)
    feats = jnp.concatenate([grads, source], 0).astype(jnp.bfloat16)
    tbar = tau_bar.reshape(tau_bar.shape[0], ncells)
    pre1 = jnp.einsum("fh,fc->hc", w_in, feats, preferred_element_type=jnp.float32) + b_in[:, None]
    hidden_one = jax.nn.silu(pre1).astype(jnp.bfloat16)
    pre2 = (
        jnp.einsum("gh,gc->hc", w_mid, hidden_one, preferred_element_type=jnp.float32)
        + b_mid[:, None]
    )
    hidden_two = jax.nn.silu(pre2).astype(jnp.bfloat16)
    stress = jnp.einsum("ho,hc->oc", w_out, hidden_two, preferred_element_type=jnp.float32)
    grad_w_out_t = jnp.einsum("oc,hc->oh", tbar, hidden_two, preferred_element_type=jnp.float32)
    back_two = jnp.einsum("ho,oc->hc", w_out, tbar, preferred_element_type=jnp.float32)
    delta_two = (back_two * dsilu(pre2)).astype(jnp.bfloat16)
    back_one = jnp.einsum("gh,hc->gc", w_mid, delta_two, preferred_element_type=jnp.float32)
    delta_one = (back_one * dsilu(pre1)).astype(jnp.bfloat16)
    grad_w_in = jnp.einsum("fc,hc->fh", feats, delta_one, preferred_element_type=jnp.float32)
    grad_b_in = jnp.sum(delta_one.astype(jnp.float32), 1)
    nz, ny = lax.axis_size("gz"), lax.axis_size("gy")
    count = nz * ny
    feats_bar = jnp.einsum("fh,hc->fc", w_in, delta_one, preferred_element_type=jnp.float32)

    def velocity_work(feats_bar):
        grads_bar = feats_bar[:9].reshape(3, 3, ncz, ncy, ncx)
        zpad = with_halo(grads_bar[:, 0], (("gz", 1),), 1)
        ypad = with_halo(grads_bar[:, 1], (("gy", 2),), 1)
        term_z = (zpad[:, 2:] - zpad[:, :-2]) * 0.5
        term_y = (ypad[:, :, 2:] - ypad[:, :, :-2]) * 0.5
        term_x = roll_diff(grads_bar[:, 2])
        return -(term_z + term_y + term_x)

    def particle_work(feats_bar, recv_cell, slot, live, rate, slip):
        per_slot = collect(feats_bar[9:12], recv_cell, ncells)
        returned = lax.all_to_all(per_slot, "gz", split_axis=1, concat_axis=1, tiled=True)
        at_particle = returned[:, slot]
        slip_bar = jnp.where(live[None, :], rate[None, :] * at_particle, 0.0)
        rate_bar = jnp.where(live, jnp.sum(slip * at_particle, 0), 0.0)
        return slip_bar, rate_bar

    steps = (count - 1).bit_length()
    row_steps = max(steps - 3, 0)
    nh = hidden_one.shape[0]
    small = jnp.concatenate([grad_w_in, grad_b_in[None], grad_w_out_t], 0)
    rows_needed = nh + 1 + small.shape[0]
    unit = 8 << row_steps
    rows_total = -(-rows_needed // unit) * unit
    left = jnp.concatenate(
        [
            hidden_one,
            jnp.ones((1, ncells), hidden_one.dtype),
            jnp.zeros((rows_total - nh - 1, ncells), hidden_one.dtype),
        ],
        0,
    )
    half = delta_two.shape[0] // 2

    def first_step(low_bit):
        def part(offset):
            right = lax.dynamic_slice_in_dim(delta_two, offset, half, 0)
            out = jnp.einsum("gc,hc->gh", left, right, preferred_element_type=jnp.float32)
            return lax.dynamic_update_slice(
                out, lax.dynamic_slice_in_dim(small, offset, half, 1), (nh + 1, 0)
            )

        return part(low_bit * half), part((1 - low_bit) * half)

    windows = {
        1: (velocity_work, (feats_bar,)),
        steps + 1: (particle_work, (feats_bar, recv_cell, slot, live, rate, slip)),
    }
    (low_part, high_part), results = tree_allreduce(None, nz, ny, windows, first_step)
    packed = jnp.concatenate([low_part, high_part], 1)
    slip_bar, rate_bar = results[steps + 1]
    velocity_bar = results[1]
    grad_w_mid = packed[:nh]
    grad_b_mid = packed[nh]
    grad_w_in = packed[nh + 1 : nh + 1 + grad_w_in.shape[0]]
    start = nh + 1 + grad_w_in.shape[0]
    grad_b_in = packed[start]
    grad_w_out = packed[start + 1 : start + 1 + grad_w_out_t.shape[0]].T
    return (
        stress.reshape(stress.shape[0], ncz, ncy, ncx),
        velocity_bar,
        slip_bar,
        rate_bar,
        grad_w_in,
        grad_b_in,
        grad_w_mid,
        grad_b_mid,
        grad_w_out,
    )


def solution(mesh):
    return jax.shard_map(
        shards,
        mesh=mesh,
        in_specs=(
            P(None, "gz", "gy", None),
            P(None, ("gz", "gy")),
            P(("gz", "gy")),
            P(("gz", "gy"), None),
            P(("gz", "gy")),
            P(("gz", "gy")),
            P(),
            P(),
            P(),
            P(),
            P(),
            P(None, "gz", "gy", None),
        ),
        out_specs=(
            P(None, "gz", "gy", None),
            P(None, "gz", "gy", None),
            P(None, ("gz", "gy")),
            P(("gz", "gy")),
            P(),
            P(),
            P(),
            P(),
            P(),
        ),
        check_vma=False,
    )
```

```python
import jax
import jax.numpy as jnp
from jax import lax
from jax.sharding import PartitionSpec as P


def with_halo(cells, sides, width):
    for axis, dim in sides:
        count = lax.axis_size(axis)
        head = lax.slice_in_dim(cells, 0, width, axis=dim)
        tail = lax.slice_in_dim(cells, cells.shape[dim] - width, cells.shape[dim], axis=dim)
        cells = jnp.concatenate(
            [
                lax.ppermute(tail, axis, [(i, (i + 1) % count) for i in range(count)]),
                cells,
                lax.ppermute(head, axis, [((i + 1) % count, i) for i in range(count)]),
            ],
            axis=dim,
        )
    return cells


def dsilu(value):
    sig = jax.nn.sigmoid(value)
    return sig * (1.0 + value * (1.0 - sig))


def deposit(forces, cell_row, ncells):
    block = min(512, ncells)
    count_blocks = ncells // block

    def deposit_one_block(index):
        start = index * block
        onehot = (
            cell_row[0][:, None] == start + jnp.arange(block, dtype=jnp.int32)[None, :]
        ).astype(jnp.float32)
        return jnp.dot(
            forces, onehot, precision=lax.Precision.HIGHEST, preferred_element_type=jnp.float32
        )

    pieces = lax.map(deposit_one_block, jnp.arange(count_blocks, dtype=jnp.int32))
    return pieces.transpose(1, 0, 2).reshape(forces.shape[0], ncells)


def collect(values, cell_row, ncells):
    block = min(512, ncells)
    count_blocks = ncells // block

    def collect_one_block(index, total):
        start = index * block
        onehot = (
            start + jnp.arange(block, dtype=jnp.int32)[:, None] == cell_row[0][None, :]
        ).astype(jnp.float32)
        return total + jnp.dot(
            values, onehot, precision=lax.Precision.HIGHEST, preferred_element_type=jnp.float32
        )

    init = jnp.zeros((values.shape[0], cell_row.shape[1]), jnp.float32)
    return lax.fori_loop(0, count_blocks, collect_one_block, init)


def tree_dims(nz, ny):
    gy_bits = [("gy", b) for b in range((ny - 1).bit_length())]
    gz_bits = [("gz", b) for b in range((nz - 1).bit_length())]
    dims = gy_bits + gz_bits
    if len(gy_bits) < 2 or not gz_bits:
        return lambda index: dims
    if len(gz_bits) < 2:
        first, second = [gy_bits[0], gy_bits[1], gz_bits[0]], [gy_bits[0], gz_bits[0], gy_bits[1]]
        rest = gy_bits[2:] + gz_bits[1:]
    else:
        first = [gy_bits[0], gy_bits[1], gz_bits[1], gz_bits[0]]
        second = [gy_bits[0], gz_bits[1], gz_bits[0], gy_bits[1]]
        rest = gy_bits[2:] + gz_bits[2:]
    return lambda index: (first if index % ny % 2 == 0 else second) + rest


def tree_allreduce(packed, nz, ny, windows, first_step):
    orders = tree_dims(nz, ny)
    count = nz * ny
    steps = len(orders(0))
    lane_steps = min(steps, 3)

    def bit(index, dim):
        row, col = divmod(index, ny)
        return ((row if dim[0] == "gz" else col) >> dim[1]) & 1

    def partner(index, dim):
        row, col = divmod(index, ny)
        if dim[0] == "gz":
            row ^= 1 << dim[1]
        else:
            col ^= 1 << dim[1]
        return row * ny + col

    me = lax.axis_index("gz") * ny + lax.axis_index("gy")
    table = jnp.array([[bit(i, orders(i)[k]) for k in range(steps)] for i in range(count)], jnp.int32)
    mine = table[me]
    pairs = [[(i, partner(i, orders(i)[k])) for i in range(count)] for k in range(steps)]
    results = {}

    def exchange(send, k, key):
        if key not in windows:
            return lax.ppermute(send, ("gz", "gy"), pairs[k])
        work, inputs = windows[key]
        send, inputs = lax.optimization_barrier((send, inputs))
        got = lax.ppermute(send, ("gz", "gy"), pairs[k])
        outputs = work(*inputs)
        got, results[key] = lax.optimization_barrier((got, outputs))
        return got

    halving = max(steps - 1, 1)
    for k in range(halving):
        axis = 1 if k < lane_steps else 0
        if k == 0:
            keep, send = first_step(mine[0])
        else:
            half = packed.shape[axis] // 2
            keep = lax.dynamic_slice_in_dim(packed, mine[k] * half, half, axis)
            send = lax.dynamic_slice_in_dim(packed, (1 - mine[k]) * half, half, axis)
        packed = keep + exchange(send, k, k)
    for k in range(halving, steps):
        packed = packed + exchange(packed, k, k)
    for k in reversed(range(1, halving)):
        axis = 1 if k < lane_steps else 0
        got = exchange(packed, k, steps + k)
        low = mine[k] == 0
        packed = jnp.concatenate(
            [jnp.where(low, packed, got), jnp.where(low, got, packed)], axis
        )
    got = exchange(packed, 0, steps)
    low = mine[0] == 0
    return (jnp.where(low, packed, got), jnp.where(low, got, packed)), results


def roll_diff(field):
    return (jnp.roll(field, -1, 3) - jnp.roll(field, 1, 3)) * 0.5


def shards(velocity, slip, rate, owner, cell, count, w_in, b_in, w_mid, b_mid, w_out, tau_bar):
    nparts = slip.shape[1]
    slabs = lax.axis_size("gz")
    capacity = 2 * nparts // slabs
    width_all = slabs * capacity
    ncz, ncy, ncx = (velocity.shape[1], velocity.shape[2], velocity.shape[3])
    ncells = ncz * ncy * ncx
    padded = with_halo(velocity, (("gz", 1), ("gy", 2)), 1)
    core = padded[:, 1:-1, 1:-1]
    along_z = (padded[:, 2:, 1:-1] - padded[:, :-2, 1:-1]) * 0.5
    along_y = (padded[:, 1:-1, 2:] - padded[:, 1:-1, :-2]) * 0.5
    grads = jnp.stack([along_z, along_y, roll_diff(core)], 1).reshape(9, ncells)
    live = jnp.arange(nparts, dtype=jnp.int32) < count[0]
    force = jnp.where(live[None, :], rate[None, :] * slip, 0.0)
    owners = owner[:, 0]
    member = (owners[:, None] == jnp.arange(slabs, dtype=jnp.int32)[None, :]).astype(jnp.int32)
    before = jnp.cumsum(member, 0) - member
    position = jnp.sum(before * member, 1)
    slot = owners * capacity + position
    payload = jnp.concatenate(
        [force, jnp.where(live, cell, -1).astype(jnp.float32)[None]], 0
    )
    base = jnp.concatenate(
        [jnp.zeros((3, width_all), jnp.float32), jnp.full((1, width_all), -1.0, jnp.float32)], 0
    )
    received = lax.all_to_all(
        base.at[:, slot].set(payload), "gz", split_axis=1, concat_axis=1, tiled=True
    )
    recv_force = received[:3]
    recv_cell = received[3:].astype(jnp.int32)
    source = deposit(recv_force, recv_cell, ncells)
    feats = jnp.concatenate([grads, source], 0).astype(jnp.bfloat16)
    tbar = tau_bar.reshape(tau_bar.shape[0], ncells)
    pre1 = jnp.einsum("fh,fc->hc", w_in, feats, preferred_element_type=jnp.float32) + b_in[:, None]
    hidden_one = jax.nn.silu(pre1).astype(jnp.bfloat16)
    pre2 = (
        jnp.einsum("gh,gc->hc", w_mid, hidden_one, preferred_element_type=jnp.float32)
        + b_mid[:, None]
    )
    hidden_two = jax.nn.silu(pre2).astype(jnp.bfloat16)
    stress = jnp.einsum("ho,hc->oc", w_out, hidden_two, preferred_element_type=jnp.float32)
    grad_w_out_t = jnp.einsum("oc,hc->oh", tbar, hidden_two, preferred_element_type=jnp.float32)
    back_two = jnp.einsum("ho,oc->hc", w_out, tbar, preferred_element_type=jnp.float32)
    delta_two = (back_two * dsilu(pre2)).astype(jnp.bfloat16)
    back_one = jnp.einsum("gh,hc->gc", w_mid, delta_two, preferred_element_type=jnp.float32)
    delta_one = (back_one * dsilu(pre1)).astype(jnp.bfloat16)
    grad_w_in = jnp.einsum("fc,hc->fh", feats, delta_one, preferred_element_type=jnp.float32)
    grad_b_in = jnp.sum(delta_one.astype(jnp.float32), 1)
    nz, ny = lax.axis_size("gz"), lax.axis_size("gy")
    count = nz * ny
    feats_bar = jnp.einsum("fh,hc->fc", w_in, delta_one, preferred_element_type=jnp.float32)

    def velocity_work(feats_bar):
        grads_bar = feats_bar[:9].reshape(3, 3, ncz, ncy, ncx)
        zpad = with_halo(grads_bar[:, 0], (("gz", 1),), 1)
        ypad = with_halo(grads_bar[:, 1], (("gy", 2),), 1)
        term_z = (zpad[:, 2:] - zpad[:, :-2]) * 0.5
        term_y = (ypad[:, :, 2:] - ypad[:, :, :-2]) * 0.5
        term_x = roll_diff(grads_bar[:, 2])
        return -(term_z + term_y + term_x)

    def particle_work(feats_bar, recv_cell, slot, live, rate, slip):
        per_slot = collect(feats_bar[9:12], recv_cell, ncells)
        returned = lax.all_to_all(per_slot, "gz", split_axis=1, concat_axis=1, tiled=True)
        at_particle = returned[:, slot]
        slip_bar = jnp.where(live[None, :], rate[None, :] * at_particle, 0.0)
        rate_bar = jnp.where(live, jnp.sum(slip * at_particle, 0), 0.0)
        return slip_bar, rate_bar

    steps = (count - 1).bit_length()
    row_steps = max(steps - 3, 0)
    nh = hidden_one.shape[0]
    small = jnp.concatenate([grad_w_in, grad_b_in[None], grad_w_out_t], 0)
    rows_needed = nh + 1 + small.shape[0]
    unit = 8 << row_steps
    rows_total = -(-rows_needed // unit) * unit
    left = jnp.concatenate(
        [
            hidden_one,
            jnp.ones((1, ncells), hidden_one.dtype),
            jnp.zeros((rows_total - nh - 1, ncells), hidden_one.dtype),
        ],
        0,
    )
    half = delta_two.shape[0] // 2

    def first_step(low_bit):
        def part(offset):
            right = lax.dynamic_slice_in_dim(delta_two, offset, half, 0)
            out = jnp.einsum("gc,hc->gh", left, right, preferred_element_type=jnp.float32)
            extra = lax.dynamic_slice_in_dim(small, offset, half, 1)
            return out + jnp.pad(extra, ((nh + 1, rows_total - rows_needed), (0, 0)))

        return part(low_bit * half), part((1 - low_bit) * half)

    windows = {
        1: (velocity_work, (feats_bar,)),
        steps + 1: (particle_work, (feats_bar, recv_cell, slot, live, rate, slip)),
    }
    (low_part, high_part), results = tree_allreduce(None, nz, ny, windows, first_step)
    packed = jnp.concatenate([low_part, high_part], 1)
    slip_bar, rate_bar = results[steps + 1]
    velocity_bar = results[1]
    grad_w_mid = packed[:nh]
    grad_b_mid = packed[nh]
    grad_w_in = packed[nh + 1 : nh + 1 + grad_w_in.shape[0]]
    start = nh + 1 + grad_w_in.shape[0]
    grad_b_in = packed[start]
    grad_w_out = packed[start + 1 : start + 1 + grad_w_out_t.shape[0]].T
    return (
        stress.reshape(stress.shape[0], ncz, ncy, ncx),
        velocity_bar,
        slip_bar,
        rate_bar,
        grad_w_in,
        grad_b_in,
        grad_w_mid,
        grad_b_mid,
        grad_w_out,
    )


def solution(mesh):
    return jax.shard_map(
        shards,
        mesh=mesh,
        in_specs=(
            P(None, "gz", "gy", None),
            P(None, ("gz", "gy")),
            P(("gz", "gy")),
            P(("gz", "gy"), None),
            P(("gz", "gy")),
            P(("gz", "gy")),
            P(),
            P(),
            P(),
            P(),
            P(),
            P(None, "gz", "gy", None),
        ),
        out_specs=(
            P(None, "gz", "gy", None),
            P(None, "gz", "gy", None),
            P(None, ("gz", "gy")),
            P(("gz", "gy")),
            P(),
            P(),
            P(),
            P(),
            P(),
        ),
        check_vma=False,
    )
```

```python
import jax
import jax.numpy as jnp
from jax import lax
from jax.sharding import PartitionSpec as P


def with_halo(cells, sides, width):
    for axis, dim in sides:
        count = lax.axis_size(axis)
        head = lax.slice_in_dim(cells, 0, width, axis=dim)
        tail = lax.slice_in_dim(cells, cells.shape[dim] - width, cells.shape[dim], axis=dim)
        cells = jnp.concatenate(
            [
                lax.ppermute(tail, axis, [(i, (i + 1) % count) for i in range(count)]),
                cells,
                lax.ppermute(head, axis, [((i + 1) % count, i) for i in range(count)]),
            ],
            axis=dim,
        )
    return cells


def dsilu(value):
    sig = jax.nn.sigmoid(value)
    return sig * (1.0 + value * (1.0 - sig))


def deposit(forces, cell_row, ncells):
    block = min(512, ncells)
    count_blocks = ncells // block

    def deposit_one_block(index):
        start = index * block
        onehot = (
            cell_row[0][:, None] == start + jnp.arange(block, dtype=jnp.int32)[None, :]
        ).astype(jnp.float32)
        return jnp.dot(
            forces, onehot, precision=lax.Precision.HIGHEST, preferred_element_type=jnp.float32
        )

    pieces = lax.map(deposit_one_block, jnp.arange(count_blocks, dtype=jnp.int32))
    return pieces.transpose(1, 0, 2).reshape(forces.shape[0], ncells)


def collect(values, cell_row, ncells):
    block = min(512, ncells)
    count_blocks = ncells // block

    def collect_one_block(index, total):
        start = index * block
        onehot = (
            start + jnp.arange(block, dtype=jnp.int32)[:, None] == cell_row[0][None, :]
        ).astype(jnp.float32)
        return total + jnp.dot(
            values, onehot, precision=lax.Precision.HIGHEST, preferred_element_type=jnp.float32
        )

    init = jnp.zeros((values.shape[0], cell_row.shape[1]), jnp.float32)
    return lax.fori_loop(0, count_blocks, collect_one_block, init)


def tree_dims(nz, ny):
    gy_bits = [("gy", b) for b in range((ny - 1).bit_length())]
    gz_bits = [("gz", b) for b in range((nz - 1).bit_length())]
    dims = gy_bits + gz_bits
    if len(gy_bits) < 2 or not gz_bits:
        return lambda index: dims
    if len(gz_bits) < 2:
        first, second = [gy_bits[0], gy_bits[1], gz_bits[0]], [gy_bits[0], gz_bits[0], gy_bits[1]]
        rest = gy_bits[2:] + gz_bits[1:]
    else:
        first = [gy_bits[0], gy_bits[1], gz_bits[1], gz_bits[0]]
        second = [gy_bits[0], gz_bits[1], gz_bits[0], gy_bits[1]]
        rest = gy_bits[2:] + gz_bits[2:]
    return lambda index: (first if index % ny % 2 == 0 else second) + rest


def tree_allreduce(packed, nz, ny, windows, first_step):
    orders = tree_dims(nz, ny)
    count = nz * ny
    steps = len(orders(0))
    lane_steps = min(steps, 3)

    def bit(index, dim):
        row, col = divmod(index, ny)
        return ((row if dim[0] == "gz" else col) >> dim[1]) & 1

    def partner(index, dim):
        row, col = divmod(index, ny)
        if dim[0] == "gz":
            row ^= 1 << dim[1]
        else:
            col ^= 1 << dim[1]
        return row * ny + col

    me = lax.axis_index("gz") * ny + lax.axis_index("gy")
    table = jnp.array([[bit(i, orders(i)[k]) for k in range(steps)] for i in range(count)], jnp.int32)
    mine = table[me]
    pairs = [[(i, partner(i, orders(i)[k])) for i in range(count)] for k in range(steps)]
    results = {}

    def exchange(send, k, key):
        if key not in windows:
            return lax.ppermute(send, ("gz", "gy"), pairs[k])
        work, inputs = windows[key]
        send, inputs = lax.optimization_barrier((send, inputs))
        got = lax.ppermute(send, ("gz", "gy"), pairs[k])
        outputs = work(*inputs)
        got, results[key] = lax.optimization_barrier((got, outputs))
        return got

    halving = max(steps - 1, 1)
    for k in range(halving):
        axis = 1 if k < lane_steps else 0
        if k == 0:
            keep, send = first_step(mine[0])
        else:
            half = packed.shape[axis] // 2
            keep = lax.dynamic_slice_in_dim(packed, mine[k] * half, half, axis)
            send = lax.dynamic_slice_in_dim(packed, (1 - mine[k]) * half, half, axis)
        packed = keep + exchange(send, k, k)
    for k in range(halving, steps):
        packed = packed + exchange(packed, k, k)
    for k in reversed(range(1, halving)):
        axis = 1 if k < lane_steps else 0
        got = exchange(packed, k, steps + k)
        low = mine[k] == 0
        packed = jnp.concatenate(
            [jnp.where(low, packed, got), jnp.where(low, got, packed)], axis
        )
    got = exchange(packed, 0, steps)
    low = mine[0] == 0
    return (jnp.where(low, packed, got), jnp.where(low, got, packed)), results


def roll_diff(field):
    return (jnp.roll(field, -1, 3) - jnp.roll(field, 1, 3)) * 0.5


def shards(velocity, slip, rate, owner, cell, count, w_in, b_in, w_mid, b_mid, w_out, tau_bar):
    nparts = slip.shape[1]
    slabs = lax.axis_size("gz")
    capacity = 2 * nparts // slabs
    width_all = slabs * capacity
    ncz, ncy, ncx = (velocity.shape[1], velocity.shape[2], velocity.shape[3])
    ncells = ncz * ncy * ncx
    padded = with_halo(velocity, (("gz", 1), ("gy", 2)), 1)
    core = padded[:, 1:-1, 1:-1]
    along_z = (padded[:, 2:, 1:-1] - padded[:, :-2, 1:-1]) * 0.5
    along_y = (padded[:, 1:-1, 2:] - padded[:, 1:-1, :-2]) * 0.5
    grads = jnp.stack([along_z, along_y, roll_diff(core)], 1).reshape(9, ncells)
    live = jnp.arange(nparts, dtype=jnp.int32) < count[0]
    force = jnp.where(live[None, :], rate[None, :] * slip, 0.0)
    owners = owner[:, 0]
    member = (owners[:, None] == jnp.arange(slabs, dtype=jnp.int32)[None, :]).astype(jnp.int32)
    before = jnp.cumsum(member, 0) - member
    position = jnp.sum(before * member, 1)
    slot = owners * capacity + position
    payload = jnp.concatenate(
        [force, jnp.where(live, cell, -1).astype(jnp.float32)[None]], 0
    )
    base = jnp.concatenate(
        [jnp.zeros((3, width_all), jnp.float32), jnp.full((1, width_all), -1.0, jnp.float32)], 0
    )
    received = lax.all_to_all(
        base.at[:, slot].set(payload), "gz", split_axis=1, concat_axis=1, tiled=True
    )
    recv_force = received[:3]
    recv_cell = received[3:].astype(jnp.int32)
    source = deposit(recv_force, recv_cell, ncells)
    feats = jnp.concatenate([grads, source], 0).astype(jnp.bfloat16)
    tbar = tau_bar.reshape(tau_bar.shape[0], ncells)
    pre1 = jnp.einsum("fh,fc->hc", w_in, feats, preferred_element_type=jnp.float32) + b_in[:, None]
    hidden_one = jax.nn.silu(pre1).astype(jnp.bfloat16)
    pre2 = (
        jnp.einsum("gh,gc->hc", w_mid, hidden_one, preferred_element_type=jnp.float32)
        + b_mid[:, None]
    )
    hidden_two = jax.nn.silu(pre2).astype(jnp.bfloat16)
    stress = jnp.einsum("ho,hc->oc", w_out, hidden_two, preferred_element_type=jnp.float32)
    grad_w_out_t = jnp.einsum("oc,hc->oh", tbar, hidden_two, preferred_element_type=jnp.float32)
    back_two = jnp.einsum("ho,oc->hc", w_out, tbar, preferred_element_type=jnp.float32)
    delta_two = (back_two * dsilu(pre2)).astype(jnp.bfloat16)
    back_one = jnp.einsum("gh,hc->gc", w_mid, delta_two, preferred_element_type=jnp.float32)
    delta_one = (back_one * dsilu(pre1)).astype(jnp.bfloat16)
    grad_w_in = jnp.einsum("fc,hc->fh", feats, delta_one, preferred_element_type=jnp.float32)
    grad_b_in = jnp.sum(delta_one.astype(jnp.float32), 1)
    nz, ny = lax.axis_size("gz"), lax.axis_size("gy")
    count = nz * ny
    feats_bar = jnp.einsum("fh,hc->fc", w_in, delta_one, preferred_element_type=jnp.float32)

    def velocity_work(feats_bar):
        grads_bar = feats_bar[:9].reshape(3, 3, ncz, ncy, ncx)
        zpad = with_halo(grads_bar[:, 0], (("gz", 1),), 1)
        ypad = with_halo(grads_bar[:, 1], (("gy", 2),), 1)
        term_z = (zpad[:, 2:] - zpad[:, :-2]) * 0.5
        term_y = (ypad[:, :, 2:] - ypad[:, :, :-2]) * 0.5
        term_x = roll_diff(grads_bar[:, 2])
        return -(term_z + term_y + term_x)

    def particle_work(feats_bar, recv_cell, slot, live, rate, slip):
        per_slot = collect(feats_bar[9:12], recv_cell, ncells)
        returned = lax.all_to_all(per_slot, "gz", split_axis=1, concat_axis=1, tiled=True)
        at_particle = returned[:, slot]
        slip_bar = jnp.where(live[None, :], rate[None, :] * at_particle, 0.0)
        rate_bar = jnp.where(live, jnp.sum(slip * at_particle, 0), 0.0)
        return slip_bar, rate_bar

    steps = (count - 1).bit_length()
    row_steps = max(steps - 3, 0)
    nh = hidden_one.shape[0]
    small = jnp.concatenate([grad_w_in, grad_b_in[None], grad_w_out_t], 0)
    rows_needed = nh + 1 + small.shape[0]
    unit = 8 << row_steps
    rows_total = -(-rows_needed // unit) * unit
    left = jnp.concatenate(
        [
            hidden_one,
            jnp.ones((1, ncells), hidden_one.dtype),
            jnp.zeros((rows_total - nh - 1, ncells), hidden_one.dtype),
        ],
        0,
    )
    half = delta_two.shape[0] // 2

    def first_step(low_bit):
        def part(offset):
            right = lax.dynamic_slice_in_dim(delta_two, offset, half, 0)
            out = jnp.einsum("gc,hc->gh", left, right, preferred_element_type=jnp.float32)
            extra = lax.dynamic_slice_in_dim(small, offset, half, 1)
            return out + jnp.pad(extra, ((nh + 1, rows_total - rows_needed), (0, 0)))

        return part(low_bit * half), part((1 - low_bit) * half)

    windows = {
        steps - 1: (velocity_work, (feats_bar,)),
        steps + 1: (particle_work, (feats_bar, recv_cell, slot, live, rate, slip)),
    }
    (low_part, high_part), results = tree_allreduce(None, nz, ny, windows, first_step)
    packed = jnp.concatenate([low_part, high_part], 1)
    slip_bar, rate_bar = results[steps + 1]
    velocity_bar = results[steps - 1]
    grad_w_mid = packed[:nh]
    grad_b_mid = packed[nh]
    grad_w_in = packed[nh + 1 : nh + 1 + grad_w_in.shape[0]]
    start = nh + 1 + grad_w_in.shape[0]
    grad_b_in = packed[start]
    grad_w_out = packed[start + 1 : start + 1 + grad_w_out_t.shape[0]].T
    return (
        stress.reshape(stress.shape[0], ncz, ncy, ncx),
        velocity_bar,
        slip_bar,
        rate_bar,
        grad_w_in,
        grad_b_in,
        grad_w_mid,
        grad_b_mid,
        grad_w_out,
    )


def solution(mesh):
    return jax.shard_map(
        shards,
        mesh=mesh,
        in_specs=(
            P(None, "gz", "gy", None),
            P(None, ("gz", "gy")),
            P(("gz", "gy")),
            P(("gz", "gy"), None),
            P(("gz", "gy")),
            P(("gz", "gy")),
            P(),
            P(),
            P(),
            P(),
            P(),
            P(None, "gz", "gy", None),
        ),
        out_specs=(
            P(None, "gz", "gy", None),
            P(None, "gz", "gy", None),
            P(None, ("gz", "gy")),
            P(("gz", "gy")),
            P(),
            P(),
            P(),
            P(),
            P(),
        ),
        check_vma=False,
    )
```

```python
import jax
import jax.numpy as jnp
from jax import lax
from jax.sharding import PartitionSpec as P


def with_halo(cells, sides, width):
    for axis, dim in sides:
        count = lax.axis_size(axis)
        head = lax.slice_in_dim(cells, 0, width, axis=dim)
        tail = lax.slice_in_dim(cells, cells.shape[dim] - width, cells.shape[dim], axis=dim)
        cells = jnp.concatenate(
            [
                lax.ppermute(tail, axis, [(i, (i + 1) % count) for i in range(count)]),
                cells,
                lax.ppermute(head, axis, [((i + 1) % count, i) for i in range(count)]),
            ],
            axis=dim,
        )
    return cells


def dsilu(value):
    sig = jax.nn.sigmoid(value)
    return sig * (1.0 + value * (1.0 - sig))


def deposit(forces, cell_row, ncells):
    block = min(512, ncells)
    count_blocks = ncells // block

    def deposit_one_block(index):
        start = index * block
        onehot = (
            cell_row[0][:, None] == start + jnp.arange(block, dtype=jnp.int32)[None, :]
        ).astype(jnp.float32)
        return jnp.dot(
            forces, onehot, precision=lax.Precision.HIGHEST, preferred_element_type=jnp.float32
        )

    pieces = lax.map(deposit_one_block, jnp.arange(count_blocks, dtype=jnp.int32))
    return pieces.transpose(1, 0, 2).reshape(forces.shape[0], ncells)


def collect(values, cell_row, ncells):
    block = min(512, ncells)
    count_blocks = ncells // block

    def collect_one_block(index, total):
        start = index * block
        onehot = (
            start + jnp.arange(block, dtype=jnp.int32)[:, None] == cell_row[0][None, :]
        ).astype(jnp.float32)
        return total + jnp.dot(
            values, onehot, precision=lax.Precision.HIGHEST, preferred_element_type=jnp.float32
        )

    init = jnp.zeros((values.shape[0], cell_row.shape[1]), jnp.float32)
    return lax.fori_loop(0, count_blocks, collect_one_block, init)


def tree_dims(nz, ny):
    gy_bits = [("gy", b) for b in range((ny - 1).bit_length())]
    gz_bits = [("gz", b) for b in range((nz - 1).bit_length())]
    dims = gy_bits + gz_bits
    if len(gy_bits) < 2 or not gz_bits:
        return lambda index: dims
    if len(gz_bits) < 2:
        first, second = [gy_bits[0], gy_bits[1], gz_bits[0]], [gy_bits[0], gz_bits[0], gy_bits[1]]
        rest = gy_bits[2:] + gz_bits[1:]
    else:
        first = [gy_bits[0], gy_bits[1], gz_bits[1], gz_bits[0]]
        second = [gy_bits[0], gz_bits[1], gz_bits[0], gy_bits[1]]
        rest = gy_bits[2:] + gz_bits[2:]
    return lambda index: (first if index % ny % 2 == 0 else second) + rest


def tree_allreduce(packed, nz, ny, windows, first_step):
    orders = tree_dims(nz, ny)
    count = nz * ny
    steps = len(orders(0))
    lane_steps = min(steps, 3)

    def bit(index, dim):
        row, col = divmod(index, ny)
        return ((row if dim[0] == "gz" else col) >> dim[1]) & 1

    def partner(index, dim):
        row, col = divmod(index, ny)
        if dim[0] == "gz":
            row ^= 1 << dim[1]
        else:
            col ^= 1 << dim[1]
        return row * ny + col

    me = lax.axis_index("gz") * ny + lax.axis_index("gy")
    table = jnp.array([[bit(i, orders(i)[k]) for k in range(steps)] for i in range(count)], jnp.int32)
    mine = table[me]
    pairs = [[(i, partner(i, orders(i)[k])) for i in range(count)] for k in range(steps)]
    results = {}

    def exchange(send, k, key):
        if key not in windows:
            return lax.ppermute(send, ("gz", "gy"), pairs[k])
        work, inputs = windows[key]
        send, inputs = lax.optimization_barrier((send, inputs))
        got = lax.ppermute(send, ("gz", "gy"), pairs[k])
        outputs = work(*inputs)
        got, results[key] = lax.optimization_barrier((got, outputs))
        return got

    halving = max(steps - 1, 1)
    for k in range(halving):
        axis = 1 if k < lane_steps else 0
        if k == 0:
            keep, send = first_step(mine[0])
        else:
            half = packed.shape[axis] // 2
            keep = lax.dynamic_slice_in_dim(packed, mine[k] * half, half, axis)
            send = lax.dynamic_slice_in_dim(packed, (1 - mine[k]) * half, half, axis)
        packed = keep + exchange(send, k, k)
    for k in range(halving, steps):
        packed = packed + exchange(packed, k, k)
    for k in reversed(range(1, halving)):
        axis = 1 if k < lane_steps else 0
        got = exchange(packed, k, steps + k)
        low = mine[k] == 0
        packed = jnp.concatenate(
            [jnp.where(low, packed, got), jnp.where(low, got, packed)], axis
        )
    got = exchange(packed, 0, steps)
    low = mine[0] == 0
    return (jnp.where(low, packed, got), jnp.where(low, got, packed)), results


def roll_diff(field):
    return (jnp.roll(field, -1, 3) - jnp.roll(field, 1, 3)) * 0.5


def shards(velocity, slip, rate, owner, cell, count, w_in, b_in, w_mid, b_mid, w_out, tau_bar):
    nparts = slip.shape[1]
    slabs = lax.axis_size("gz")
    capacity = 2 * nparts // slabs
    width_all = slabs * capacity
    ncz, ncy, ncx = (velocity.shape[1], velocity.shape[2], velocity.shape[3])
    ncells = ncz * ncy * ncx
    padded = with_halo(velocity, (("gz", 1), ("gy", 2)), 1)
    core = padded[:, 1:-1, 1:-1]
    along_z = (padded[:, 2:, 1:-1] - padded[:, :-2, 1:-1]) * 0.5
    along_y = (padded[:, 1:-1, 2:] - padded[:, 1:-1, :-2]) * 0.5
    grads = jnp.stack([along_z, along_y, roll_diff(core)], 1).reshape(9, ncells)
    live = jnp.arange(nparts, dtype=jnp.int32) < count[0]
    force = jnp.where(live[None, :], rate[None, :] * slip, 0.0)
    owners = owner[:, 0]
    member = (owners[:, None] == jnp.arange(slabs, dtype=jnp.int32)[None, :]).astype(jnp.int32)
    before = jnp.cumsum(member, 0) - member
    position = jnp.sum(before * member, 1)
    slot = owners * capacity + position
    payload = jnp.concatenate(
        [force, jnp.where(live, cell, -1).astype(jnp.float32)[None]], 0
    )
    base = jnp.concatenate(
        [jnp.zeros((3, width_all), jnp.float32), jnp.full((1, width_all), -1.0, jnp.float32)], 0
    )
    received = lax.all_to_all(
        base.at[:, slot].set(payload), "gz", split_axis=1, concat_axis=1, tiled=True
    )
    recv_force = received[:3]
    recv_cell = received[3:].astype(jnp.int32)
    source = deposit(recv_force, recv_cell, ncells)
    feats = jnp.concatenate([grads, source], 0).astype(jnp.bfloat16)
    tbar = tau_bar.reshape(tau_bar.shape[0], ncells)
    pre1 = jnp.einsum("fh,fc->hc", w_in, feats, preferred_element_type=jnp.float32) + b_in[:, None]
    hidden_one = jax.nn.silu(pre1).astype(jnp.bfloat16)
    pre2 = (
        jnp.einsum("gh,gc->hc", w_mid, hidden_one, preferred_element_type=jnp.float32)
        + b_mid[:, None]
    )
    hidden_two = jax.nn.silu(pre2).astype(jnp.bfloat16)
    stress = jnp.einsum("ho,hc->oc", w_out, hidden_two, preferred_element_type=jnp.float32)
    grad_w_out_t = jnp.einsum("oc,hc->oh", tbar, hidden_two, preferred_element_type=jnp.float32)
    back_two = jnp.einsum("ho,oc->hc", w_out, tbar, preferred_element_type=jnp.float32)
    delta_two = (back_two * dsilu(pre2)).astype(jnp.bfloat16)
    back_one = jnp.einsum("gh,hc->gc", w_mid, delta_two, preferred_element_type=jnp.float32)
    delta_one = (back_one * dsilu(pre1)).astype(jnp.bfloat16)
    grad_w_in = jnp.einsum("fc,hc->fh", feats, delta_one, preferred_element_type=jnp.float32)
    grad_b_in = jnp.sum(delta_one.astype(jnp.float32), 1)
    nz, ny = lax.axis_size("gz"), lax.axis_size("gy")
    count = nz * ny
    feats_bar = jnp.einsum("fh,hc->fc", w_in, delta_one, preferred_element_type=jnp.float32)

    def velocity_work(feats_bar):
        grads_bar = feats_bar[:9].reshape(3, 3, ncz, ncy, ncx)
        zpad = with_halo(grads_bar[:, 0], (("gz", 1),), 1)
        ypad = with_halo(grads_bar[:, 1], (("gy", 2),), 1)
        term_z = (zpad[:, 2:] - zpad[:, :-2]) * 0.5
        term_y = (ypad[:, :, 2:] - ypad[:, :, :-2]) * 0.5
        term_x = roll_diff(grads_bar[:, 2])
        return -(term_z + term_y + term_x)

    def particle_work(feats_bar, recv_cell, slot, live, rate, slip):
        per_slot = collect(feats_bar[9:12], recv_cell, ncells)
        returned = lax.all_to_all(per_slot, "gz", split_axis=1, concat_axis=1, tiled=True)
        at_particle = returned[:, slot]
        slip_bar = jnp.where(live[None, :], rate[None, :] * at_particle, 0.0)
        rate_bar = jnp.where(live, jnp.sum(slip * at_particle, 0), 0.0)
        return slip_bar, rate_bar

    steps = (count - 1).bit_length()
    row_steps = max(steps - 3, 0)
    nh = hidden_one.shape[0]
    small = jnp.concatenate([grad_w_in, grad_b_in[None], grad_w_out_t], 0)
    rows_needed = nh + 1 + small.shape[0]
    unit = 8 << row_steps
    rows_total = -(-rows_needed // unit) * unit
    left = jnp.concatenate(
        [
            hidden_one,
            jnp.ones((1, ncells), hidden_one.dtype),
            jnp.zeros((rows_total - nh - 1, ncells), hidden_one.dtype),
        ],
        0,
    )
    half = delta_two.shape[0] // 2

    def first_step(low_bit):
        def part(offset):
            right = lax.dynamic_slice_in_dim(delta_two, offset, half, 0)
            out = jnp.einsum("gc,hc->gh", left, right, preferred_element_type=jnp.float32)
            extra = lax.dynamic_slice_in_dim(small, offset, half, 1)
            return out + jnp.pad(extra, ((nh + 1, rows_total - rows_needed), (0, 0)))

        return part(low_bit * half), part((1 - low_bit) * half)

    windows = {
        0: (velocity_work, (feats_bar,)),
        steps + 1: (particle_work, (feats_bar, recv_cell, slot, live, rate, slip)),
    }
    (low_part, high_part), results = tree_allreduce(None, nz, ny, windows, first_step)
    packed = jnp.concatenate([low_part, high_part], 1)
    slip_bar, rate_bar = results[steps + 1]
    velocity_bar = results[0]
    grad_w_mid = packed[:nh]
    grad_b_mid = packed[nh]
    grad_w_in = packed[nh + 1 : nh + 1 + grad_w_in.shape[0]]
    start = nh + 1 + grad_w_in.shape[0]
    grad_b_in = packed[start]
    grad_w_out = packed[start + 1 : start + 1 + grad_w_out_t.shape[0]].T
    return (
        stress.reshape(stress.shape[0], ncz, ncy, ncx),
        velocity_bar,
        slip_bar,
        rate_bar,
        grad_w_in,
        grad_b_in,
        grad_w_mid,
        grad_b_mid,
        grad_w_out,
    )


def solution(mesh):
    return jax.shard_map(
        shards,
        mesh=mesh,
        in_specs=(
            P(None, "gz", "gy", None),
            P(None, ("gz", "gy")),
            P(("gz", "gy")),
            P(("gz", "gy"), None),
            P(("gz", "gy")),
            P(("gz", "gy")),
            P(),
            P(),
            P(),
            P(),
            P(),
            P(None, "gz", "gy", None),
        ),
        out_specs=(
            P(None, "gz", "gy", None),
            P(None, "gz", "gy", None),
            P(None, ("gz", "gy")),
            P(("gz", "gy")),
            P(),
            P(),
            P(),
            P(),
            P(),
        ),
        check_vma=False,
    )
```

```python
import jax
import jax.numpy as jnp
from jax import lax
from jax.sharding import PartitionSpec as P


def with_halo(cells, sides, width):
    for axis, dim in sides:
        count = lax.axis_size(axis)
        head = lax.slice_in_dim(cells, 0, width, axis=dim)
        tail = lax.slice_in_dim(cells, cells.shape[dim] - width, cells.shape[dim], axis=dim)
        cells = jnp.concatenate(
            [
                lax.ppermute(tail, axis, [(i, (i + 1) % count) for i in range(count)]),
                cells,
                lax.ppermute(head, axis, [((i + 1) % count, i) for i in range(count)]),
            ],
            axis=dim,
        )
    return cells


def dsilu(value):
    sig = jax.nn.sigmoid(value)
    return sig * (1.0 + value * (1.0 - sig))


def deposit(forces, cell_row, ncells):
    block = min(512, ncells)
    count_blocks = ncells // block

    def deposit_one_block(index):
        start = index * block
        onehot = (
            cell_row[0][:, None] == start + jnp.arange(block, dtype=jnp.int32)[None, :]
        ).astype(jnp.float32)
        return jnp.dot(
            forces, onehot, precision=lax.Precision.HIGHEST, preferred_element_type=jnp.float32
        )

    pieces = lax.map(deposit_one_block, jnp.arange(count_blocks, dtype=jnp.int32))
    return pieces.transpose(1, 0, 2).reshape(forces.shape[0], ncells)


def collect(values, cell_row, ncells):
    block = min(512, ncells)
    count_blocks = ncells // block

    def collect_one_block(index, total):
        start = index * block
        onehot = (
            start + jnp.arange(block, dtype=jnp.int32)[:, None] == cell_row[0][None, :]
        ).astype(jnp.float32)
        return total + jnp.dot(
            values, onehot, precision=lax.Precision.HIGHEST, preferred_element_type=jnp.float32
        )

    init = jnp.zeros((values.shape[0], cell_row.shape[1]), jnp.float32)
    return lax.fori_loop(0, count_blocks, collect_one_block, init)


def tree_dims(nz, ny):
    gy_bits = [("gy", b) for b in range((ny - 1).bit_length())]
    gz_bits = [("gz", b) for b in range((nz - 1).bit_length())]
    dims = gy_bits + gz_bits
    if len(gy_bits) < 2 or not gz_bits:
        return lambda index: dims
    if len(gz_bits) < 2:
        first, second = [gy_bits[0], gy_bits[1], gz_bits[0]], [gy_bits[0], gz_bits[0], gy_bits[1]]
        rest = gy_bits[2:] + gz_bits[1:]
    else:
        first = [gy_bits[0], gy_bits[1], gz_bits[1], gz_bits[0]]
        second = [gy_bits[0], gz_bits[1], gz_bits[0], gy_bits[1]]
        rest = gy_bits[2:] + gz_bits[2:]
    return lambda index: (first if index % ny % 2 == 0 else second) + rest


def tree_allreduce(packed, nz, ny, windows, first_step):
    orders = tree_dims(nz, ny)
    count = nz * ny
    steps = len(orders(0))
    lane_steps = min(steps, 3)

    def bit(index, dim):
        row, col = divmod(index, ny)
        return ((row if dim[0] == "gz" else col) >> dim[1]) & 1

    def partner(index, dim):
        row, col = divmod(index, ny)
        if dim[0] == "gz":
            row ^= 1 << dim[1]
        else:
            col ^= 1 << dim[1]
        return row * ny + col

    me = lax.axis_index("gz") * ny + lax.axis_index("gy")
    table = jnp.array([[bit(i, orders(i)[k]) for k in range(steps)] for i in range(count)], jnp.int32)
    mine = table[me]
    pairs = [[(i, partner(i, orders(i)[k])) for i in range(count)] for k in range(steps)]
    results = {}

    def exchange(send, k, key):
        if key not in windows:
            return lax.ppermute(send, ("gz", "gy"), pairs[k])
        work, inputs = windows[key]
        send, inputs = lax.optimization_barrier((send, inputs))
        got = lax.ppermute(send, ("gz", "gy"), pairs[k])
        outputs = work(*inputs)
        got, results[key] = lax.optimization_barrier((got, outputs))
        return got

    halving = max(steps - 1, 1)
    for k in range(halving):
        axis = 1 if k < lane_steps else 0
        if k == 0:
            keep, send = first_step(mine[0])
        else:
            half = packed.shape[axis] // 2
            keep = lax.dynamic_slice_in_dim(packed, mine[k] * half, half, axis)
            send = lax.dynamic_slice_in_dim(packed, (1 - mine[k]) * half, half, axis)
        packed = keep + exchange(send, k, k)
    for k in range(halving, steps):
        packed = packed + exchange(packed, k, k)
    for k in reversed(range(1, halving)):
        axis = 1 if k < lane_steps else 0
        got = exchange(packed, k, steps + k)
        low = mine[k] == 0
        packed = jnp.concatenate(
            [jnp.where(low, packed, got), jnp.where(low, got, packed)], axis
        )
    got = exchange(packed, 0, steps)
    low = mine[0] == 0
    return (jnp.where(low, packed, got), jnp.where(low, got, packed)), results


def roll_diff(field):
    return (jnp.roll(field, -1, 3) - jnp.roll(field, 1, 3)) * 0.5


def shards(velocity, slip, rate, owner, cell, count, w_in, b_in, w_mid, b_mid, w_out, tau_bar):
    nparts = slip.shape[1]
    slabs = lax.axis_size("gz")
    capacity = 2 * nparts // slabs
    width_all = slabs * capacity
    ncz, ncy, ncx = (velocity.shape[1], velocity.shape[2], velocity.shape[3])
    ncells = ncz * ncy * ncx
    padded = with_halo(velocity, (("gz", 1), ("gy", 2)), 1)
    core = padded[:, 1:-1, 1:-1]
    along_z = (padded[:, 2:, 1:-1] - padded[:, :-2, 1:-1]) * 0.5
    along_y = (padded[:, 1:-1, 2:] - padded[:, 1:-1, :-2]) * 0.5
    grads = jnp.stack([along_z, along_y, roll_diff(core)], 1).reshape(9, ncells)
    live = jnp.arange(nparts, dtype=jnp.int32) < count[0]
    force = jnp.where(live[None, :], rate[None, :] * slip, 0.0)
    owners = owner[:, 0]
    member = (owners[:, None] == jnp.arange(slabs, dtype=jnp.int32)[None, :]).astype(jnp.int32)
    before = jnp.cumsum(member, 0) - member
    position = jnp.sum(before * member, 1)
    slot = owners * capacity + position
    payload = jnp.concatenate(
        [force, jnp.where(live, cell, -1).astype(jnp.float32)[None]], 0
    )
    base = jnp.concatenate(
        [jnp.zeros((3, width_all), jnp.float32), jnp.full((1, width_all), -1.0, jnp.float32)], 0
    )
    received = lax.all_to_all(
        base.at[:, slot].set(payload), "gz", split_axis=1, concat_axis=1, tiled=True
    )
    recv_force = received[:3]
    recv_cell = received[3:].astype(jnp.int32)
    source = deposit(recv_force, recv_cell, ncells)
    feats = jnp.concatenate([grads, source], 0).astype(jnp.bfloat16)
    tbar = tau_bar.reshape(tau_bar.shape[0], ncells)
    pre1 = jnp.einsum("fh,fc->hc", w_in, feats, preferred_element_type=jnp.float32) + b_in[:, None]
    hidden_one = jax.nn.silu(pre1).astype(jnp.bfloat16)
    pre2 = (
        jnp.einsum("gh,gc->hc", w_mid, hidden_one, preferred_element_type=jnp.float32)
        + b_mid[:, None]
    )
    hidden_two = jax.nn.silu(pre2).astype(jnp.bfloat16)
    stress = jnp.einsum("ho,hc->oc", w_out, hidden_two, preferred_element_type=jnp.float32)
    grad_w_out_t = jnp.einsum("oc,hc->oh", tbar, hidden_two, preferred_element_type=jnp.float32)
    back_two = jnp.einsum("ho,oc->hc", w_out, tbar, preferred_element_type=jnp.float32)
    delta_two = (back_two * dsilu(pre2)).astype(jnp.bfloat16)
    back_one = jnp.einsum("gh,hc->gc", w_mid, delta_two, preferred_element_type=jnp.float32)
    delta_one = (back_one * dsilu(pre1)).astype(jnp.bfloat16)
    grad_w_in = jnp.einsum("fc,hc->fh", feats, delta_one, preferred_element_type=jnp.float32)
    grad_b_in = jnp.sum(delta_one.astype(jnp.float32), 1)
    nz, ny = lax.axis_size("gz"), lax.axis_size("gy")
    count = nz * ny
    feats_bar = jnp.einsum("fh,hc->fc", w_in, delta_one, preferred_element_type=jnp.float32)

    def velocity_work(feats_bar):
        grads_bar = feats_bar[:9].reshape(3, 3, ncz, ncy, ncx)
        zpad = with_halo(grads_bar[:, 0], (("gz", 1),), 1)
        ypad = with_halo(grads_bar[:, 1], (("gy", 2),), 1)
        term_z = (zpad[:, 2:] - zpad[:, :-2]) * 0.5
        term_y = (ypad[:, :, 2:] - ypad[:, :, :-2]) * 0.5
        term_x = roll_diff(grads_bar[:, 2])
        return -(term_z + term_y + term_x)

    def particle_work(feats_bar, recv_cell, slot, live, rate, slip):
        per_slot = collect(feats_bar[9:12], recv_cell, ncells)
        returned = lax.all_to_all(per_slot, "gz", split_axis=1, concat_axis=1, tiled=True)
        at_particle = returned[:, slot]
        slip_bar = jnp.where(live[None, :], rate[None, :] * at_particle, 0.0)
        rate_bar = jnp.where(live, jnp.sum(slip * at_particle, 0), 0.0)
        return slip_bar, rate_bar

    steps = (count - 1).bit_length()
    row_steps = max(steps - 3, 0)
    nh = hidden_one.shape[0]
    grad_b_mid = jnp.sum(delta_two.astype(jnp.float32), 1)
    small = jnp.concatenate([grad_b_mid[None], grad_w_in, grad_b_in[None], grad_w_out_t], 0)
    rows_needed = nh + small.shape[0]
    unit = 8 << row_steps
    rows_total = -(-rows_needed // unit) * unit
    left = jnp.pad(hidden_one, ((0, rows_total - nh), (0, 0)))
    half = delta_two.shape[0] // 2

    def first_step(low_bit):
        def part(offset):
            right = lax.dynamic_slice_in_dim(delta_two, offset, half, 0)
            out = jnp.einsum("gc,hc->gh", left, right, preferred_element_type=jnp.float32)
            extra = lax.dynamic_slice_in_dim(small, offset, half, 1)
            return out + jnp.pad(extra, ((nh, rows_total - rows_needed), (0, 0)))

        return part(low_bit * half), part((1 - low_bit) * half)

    windows = {
        1: (velocity_work, (feats_bar,)),
        steps + 1: (particle_work, (feats_bar, recv_cell, slot, live, rate, slip)),
    }
    (low_part, high_part), results = tree_allreduce(None, nz, ny, windows, first_step)
    packed = jnp.concatenate([low_part, high_part], 1)
    slip_bar, rate_bar = results[steps + 1]
    velocity_bar = results[1]
    grad_w_mid = packed[:nh]
    grad_b_mid = packed[nh]
    grad_w_in = packed[nh + 1 : nh + 1 + grad_w_in.shape[0]]
    start = nh + 1 + grad_w_in.shape[0]
    grad_b_in = packed[start]
    grad_w_out = packed[start + 1 : start + 1 + grad_w_out_t.shape[0]].T
    return (
        stress.reshape(stress.shape[0], ncz, ncy, ncx),
        velocity_bar,
        slip_bar,
        rate_bar,
        grad_w_in,
        grad_b_in,
        grad_w_mid,
        grad_b_mid,
        grad_w_out,
    )


def solution(mesh):
    return jax.shard_map(
        shards,
        mesh=mesh,
        in_specs=(
            P(None, "gz", "gy", None),
            P(None, ("gz", "gy")),
            P(("gz", "gy")),
            P(("gz", "gy"), None),
            P(("gz", "gy")),
            P(("gz", "gy")),
            P(),
            P(),
            P(),
            P(),
            P(),
            P(None, "gz", "gy", None),
        ),
        out_specs=(
            P(None, "gz", "gy", None),
            P(None, "gz", "gy", None),
            P(None, ("gz", "gy")),
            P(("gz", "gy")),
            P(),
            P(),
            P(),
            P(),
            P(),
        ),
        check_vma=False,
    )
```

```python
import jax
import jax.numpy as jnp
from jax import lax
from jax.sharding import PartitionSpec as P


def with_halo(cells, sides, width):
    for axis, dim in sides:
        count = lax.axis_size(axis)
        head = lax.slice_in_dim(cells, 0, width, axis=dim)
        tail = lax.slice_in_dim(cells, cells.shape[dim] - width, cells.shape[dim], axis=dim)
        cells = jnp.concatenate(
            [
                lax.ppermute(tail, axis, [(i, (i + 1) % count) for i in range(count)]),
                cells,
                lax.ppermute(head, axis, [((i + 1) % count, i) for i in range(count)]),
            ],
            axis=dim,
        )
    return cells


def dsilu(value):
    sig = jax.nn.sigmoid(value)
    return sig * (1.0 + value * (1.0 - sig))


def deposit(forces, cell_row, ncells):
    block = min(512, ncells)
    count_blocks = ncells // block

    def deposit_one_block(index):
        start = index * block
        onehot = (
            cell_row[0][:, None] == start + jnp.arange(block, dtype=jnp.int32)[None, :]
        ).astype(jnp.float32)
        return jnp.dot(
            forces, onehot, precision=lax.Precision.HIGHEST, preferred_element_type=jnp.float32
        )

    pieces = lax.map(deposit_one_block, jnp.arange(count_blocks, dtype=jnp.int32))
    return pieces.transpose(1, 0, 2).reshape(forces.shape[0], ncells)


def collect(values, cell_row, ncells):
    block = min(512, ncells)
    count_blocks = ncells // block

    def collect_one_block(index, total):
        start = index * block
        onehot = (
            start + jnp.arange(block, dtype=jnp.int32)[:, None] == cell_row[0][None, :]
        ).astype(jnp.float32)
        return total + jnp.dot(
            values, onehot, precision=lax.Precision.HIGHEST, preferred_element_type=jnp.float32
        )

    init = jnp.zeros((values.shape[0], cell_row.shape[1]), jnp.float32)
    return lax.fori_loop(0, count_blocks, collect_one_block, init)


def tree_dims(nz, ny):
    gy_bits = [("gy", b) for b in range((ny - 1).bit_length())]
    gz_bits = [("gz", b) for b in range((nz - 1).bit_length())]
    dims = gy_bits + gz_bits
    if len(gy_bits) < 2 or not gz_bits:
        return lambda index: dims
    if len(gz_bits) < 2:
        first, second = [gy_bits[0], gy_bits[1], gz_bits[0]], [gy_bits[0], gz_bits[0], gy_bits[1]]
        rest = gy_bits[2:] + gz_bits[1:]
    else:
        first = [gy_bits[0], gy_bits[1], gz_bits[1], gz_bits[0]]
        second = [gy_bits[0], gz_bits[1], gz_bits[0], gy_bits[1]]
        rest = gy_bits[2:] + gz_bits[2:]
    return lambda index: (first if index % ny % 2 == 0 else second) + rest


def tree_allreduce(packed, nz, ny, windows, first_step):
    orders = tree_dims(nz, ny)
    count = nz * ny
    steps = len(orders(0))
    lane_steps = min(steps, 3)

    def bit(index, dim):
        row, col = divmod(index, ny)
        return ((row if dim[0] == "gz" else col) >> dim[1]) & 1

    def partner(index, dim):
        row, col = divmod(index, ny)
        if dim[0] == "gz":
            row ^= 1 << dim[1]
        else:
            col ^= 1 << dim[1]
        return row * ny + col

    me = lax.axis_index("gz") * ny + lax.axis_index("gy")
    table = jnp.array([[bit(i, orders(i)[k]) for k in range(steps)] for i in range(count)], jnp.int32)
    mine = table[me]
    pairs = [[(i, partner(i, orders(i)[k])) for i in range(count)] for k in range(steps)]
    results = {}

    def exchange(send, k, key):
        if key not in windows:
            return lax.ppermute(send, ("gz", "gy"), pairs[k])
        work, inputs = windows[key]
        send, inputs = lax.optimization_barrier((send, inputs))
        got = lax.ppermute(send, ("gz", "gy"), pairs[k])
        outputs = work(*inputs)
        got, results[key] = lax.optimization_barrier((got, outputs))
        return got

    halving = max(steps - 1, 1)
    for k in range(halving):
        axis = 1 if k < lane_steps else 0
        if k == 0:
            keep, send = first_step(mine[0])
        else:
            half = packed.shape[axis] // 2
            keep = lax.dynamic_slice_in_dim(packed, mine[k] * half, half, axis)
            send = lax.dynamic_slice_in_dim(packed, (1 - mine[k]) * half, half, axis)
        packed = keep + exchange(send, k, k)
    for k in range(halving, steps):
        packed = packed + exchange(packed, k, k)
    for k in reversed(range(1, halving)):
        axis = 1 if k < lane_steps else 0
        got = exchange(packed, k, steps + k)
        low = mine[k] == 0
        packed = jnp.concatenate(
            [jnp.where(low, packed, got), jnp.where(low, got, packed)], axis
        )
    got = exchange(packed, 0, steps)
    low = mine[0] == 0
    return (jnp.where(low, packed, got), jnp.where(low, got, packed)), results


def roll_diff(field):
    return (jnp.roll(field, -1, 3) - jnp.roll(field, 1, 3)) * 0.5


def shards(velocity, slip, rate, owner, cell, count, w_in, b_in, w_mid, b_mid, w_out, tau_bar):
    nparts = slip.shape[1]
    slabs = lax.axis_size("gz")
    capacity = 2 * nparts // slabs
    width_all = slabs * capacity
    ncz, ncy, ncx = (velocity.shape[1], velocity.shape[2], velocity.shape[3])
    ncells = ncz * ncy * ncx
    padded = with_halo(velocity, (("gz", 1), ("gy", 2)), 1)
    core = padded[:, 1:-1, 1:-1]
    along_z = (padded[:, 2:, 1:-1] - padded[:, :-2, 1:-1]) * 0.5
    along_y = (padded[:, 1:-1, 2:] - padded[:, 1:-1, :-2]) * 0.5
    grads = jnp.stack([along_z, along_y, roll_diff(core)], 1).reshape(9, ncells)
    live = jnp.arange(nparts, dtype=jnp.int32) < count[0]
    force = jnp.where(live[None, :], rate[None, :] * slip, 0.0)
    owners = owner[:, 0]
    member = (owners[:, None] == jnp.arange(slabs, dtype=jnp.int32)[None, :]).astype(jnp.int32)
    before = jnp.cumsum(member, 0) - member
    position = jnp.sum(before * member, 1)
    slot = owners * capacity + position
    payload = jnp.concatenate(
        [force, jnp.where(live, cell, -1).astype(jnp.float32)[None]], 0
    )
    base = jnp.concatenate(
        [jnp.zeros((3, width_all), jnp.float32), jnp.full((1, width_all), -1.0, jnp.float32)], 0
    )
    received = lax.all_to_all(
        base.at[:, slot].set(payload), "gz", split_axis=1, concat_axis=1, tiled=True
    )
    recv_force = received[:3]
    recv_cell = received[3:].astype(jnp.int32)
    source = deposit(recv_force, recv_cell, ncells)
    feats = jnp.concatenate([grads, source], 0).astype(jnp.bfloat16)
    tbar = tau_bar.reshape(tau_bar.shape[0], ncells)
    pre1 = jnp.einsum("fh,fc->hc", w_in, feats, preferred_element_type=jnp.float32) + b_in[:, None]
    hidden_one = jax.nn.silu(pre1).astype(jnp.bfloat16)
    pre2 = (
        jnp.einsum("gh,gc->hc", w_mid, hidden_one, preferred_element_type=jnp.float32)
        + b_mid[:, None]
    )
    hidden_two = jax.nn.silu(pre2).astype(jnp.bfloat16)
    stress = jnp.einsum("ho,hc->oc", w_out, hidden_two, preferred_element_type=jnp.float32)
    grad_w_out_t = jnp.einsum("oc,hc->oh", tbar, hidden_two, preferred_element_type=jnp.float32)
    back_two = jnp.einsum("ho,oc->hc", w_out, tbar, preferred_element_type=jnp.float32)
    delta_two = (back_two * dsilu(pre2)).astype(jnp.bfloat16)
    back_one = jnp.einsum("gh,hc->gc", w_mid, delta_two, preferred_element_type=jnp.float32)
    delta_one = (back_one * dsilu(pre1)).astype(jnp.bfloat16)
    grad_w_in = jnp.einsum("fc,hc->fh", feats, delta_one, preferred_element_type=jnp.float32)
    grad_b_in = jnp.sum(delta_one.astype(jnp.float32), 1)
    nz, ny = lax.axis_size("gz"), lax.axis_size("gy")
    count = nz * ny
    feats_bar = jnp.einsum("fh,hc->fc", w_in, delta_one, preferred_element_type=jnp.float32)

    def z_work(feats_bar):
        grads_bar = feats_bar[:9].reshape(3, 3, ncz, ncy, ncx)
        zpad = with_halo(grads_bar[:, 0], (("gz", 1),), 1)
        return (zpad[:, 2:] - zpad[:, :-2]) * 0.5

    def y_work(feats_bar):
        grads_bar = feats_bar[:9].reshape(3, 3, ncz, ncy, ncx)
        ypad = with_halo(grads_bar[:, 1], (("gy", 2),), 1)
        return (ypad[:, :, 2:] - ypad[:, :, :-2]) * 0.5

    def particle_work(feats_bar, recv_cell, slot, live, rate, slip):
        per_slot = collect(feats_bar[9:12], recv_cell, ncells)
        returned = lax.all_to_all(per_slot, "gz", split_axis=1, concat_axis=1, tiled=True)
        at_particle = returned[:, slot]
        slip_bar = jnp.where(live[None, :], rate[None, :] * at_particle, 0.0)
        rate_bar = jnp.where(live, jnp.sum(slip * at_particle, 0), 0.0)
        return slip_bar, rate_bar

    steps = (count - 1).bit_length()
    row_steps = max(steps - 3, 0)
    nh = hidden_one.shape[0]
    grad_b_mid = jnp.sum(delta_two.astype(jnp.float32), 1)
    small = jnp.concatenate([grad_b_mid[None], grad_w_in, grad_b_in[None], grad_w_out_t], 0)
    rows_needed = nh + small.shape[0]
    unit = 8 << row_steps
    rows_total = -(-rows_needed // unit) * unit
    left = jnp.pad(hidden_one, ((0, rows_total - nh), (0, 0)))
    half = delta_two.shape[0] // 2

    def first_step(low_bit):
        def part(offset):
            right = lax.dynamic_slice_in_dim(delta_two, offset, half, 0)
            out = jnp.einsum("gc,hc->gh", left, right, preferred_element_type=jnp.float32)
            extra = lax.dynamic_slice_in_dim(small, offset, half, 1)
            return out + jnp.pad(extra, ((nh, rows_total - rows_needed), (0, 0)))

        return part(low_bit * half), part((1 - low_bit) * half)

    windows = {
        1: (z_work, (feats_bar,)),
        2: (y_work, (feats_bar,)),
        steps + 1: (particle_work, (feats_bar, recv_cell, slot, live, rate, slip)),
    }
    (low_part, high_part), results = tree_allreduce(None, nz, ny, windows, first_step)
    packed = jnp.concatenate([low_part, high_part], 1)
    slip_bar, rate_bar = results[steps + 1]
    term_x = roll_diff(feats_bar[:9].reshape(3, 3, ncz, ncy, ncx)[:, 2])
    velocity_bar = -(results[1] + results[2] + term_x)
    grad_w_mid = packed[:nh]
    grad_b_mid = packed[nh]
    grad_w_in = packed[nh + 1 : nh + 1 + grad_w_in.shape[0]]
    start = nh + 1 + grad_w_in.shape[0]
    grad_b_in = packed[start]
    grad_w_out = packed[start + 1 : start + 1 + grad_w_out_t.shape[0]].T
    return (
        stress.reshape(stress.shape[0], ncz, ncy, ncx),
        velocity_bar,
        slip_bar,
        rate_bar,
        grad_w_in,
        grad_b_in,
        grad_w_mid,
        grad_b_mid,
        grad_w_out,
    )


def solution(mesh):
    return jax.shard_map(
        shards,
        mesh=mesh,
        in_specs=(
            P(None, "gz", "gy", None),
            P(None, ("gz", "gy")),
            P(("gz", "gy")),
            P(("gz", "gy"), None),
            P(("gz", "gy")),
            P(("gz", "gy")),
            P(),
            P(),
            P(),
            P(),
            P(),
            P(None, "gz", "gy", None),
        ),
        out_specs=(
            P(None, "gz", "gy", None),
            P(None, "gz", "gy", None),
            P(None, ("gz", "gy")),
            P(("gz", "gy")),
            P(),
            P(),
            P(),
            P(),
            P(),
        ),
        check_vma=False,
    )
```

```python
import jax
import jax.numpy as jnp
from jax import lax
from jax.sharding import PartitionSpec as P


def with_halo(cells, sides, width):
    for axis, dim in sides:
        count = lax.axis_size(axis)
        head = lax.slice_in_dim(cells, 0, width, axis=dim)
        tail = lax.slice_in_dim(cells, cells.shape[dim] - width, cells.shape[dim], axis=dim)
        cells = jnp.concatenate(
            [
                lax.ppermute(tail, axis, [(i, (i + 1) % count) for i in range(count)]),
                cells,
                lax.ppermute(head, axis, [((i + 1) % count, i) for i in range(count)]),
            ],
            axis=dim,
        )
    return cells


def dsilu(value):
    sig = jax.nn.sigmoid(value)
    return sig * (1.0 + value * (1.0 - sig))


def deposit(forces, cell_row, ncells):
    block = min(512, ncells)
    count_blocks = ncells // block

    def deposit_one_block(index):
        start = index * block
        onehot = (
            cell_row[0][:, None] == start + jnp.arange(block, dtype=jnp.int32)[None, :]
        ).astype(jnp.float32)
        return jnp.dot(
            forces, onehot, precision=lax.Precision.HIGHEST, preferred_element_type=jnp.float32
        )

    pieces = lax.map(deposit_one_block, jnp.arange(count_blocks, dtype=jnp.int32))
    return pieces.transpose(1, 0, 2).reshape(forces.shape[0], ncells)


def collect(values, cell_row, ncells):
    block = min(512, ncells)
    count_blocks = ncells // block

    def collect_one_block(index, total):
        start = index * block
        onehot = (
            start + jnp.arange(block, dtype=jnp.int32)[:, None] == cell_row[0][None, :]
        ).astype(jnp.float32)
        return total + jnp.dot(
            values, onehot, precision=lax.Precision.HIGHEST, preferred_element_type=jnp.float32
        )

    init = jnp.zeros((values.shape[0], cell_row.shape[1]), jnp.float32)
    return lax.fori_loop(0, count_blocks, collect_one_block, init)


def tree_dims(nz, ny):
    gy_bits = [("gy", b) for b in range((ny - 1).bit_length())]
    gz_bits = [("gz", b) for b in range((nz - 1).bit_length())]
    dims = gy_bits + gz_bits
    if len(gy_bits) < 2 or not gz_bits:
        return lambda index: dims
    if len(gz_bits) < 2:
        first, second = [gy_bits[0], gy_bits[1], gz_bits[0]], [gy_bits[0], gz_bits[0], gy_bits[1]]
        rest = gy_bits[2:] + gz_bits[1:]
    else:
        first = [gy_bits[0], gy_bits[1], gz_bits[1], gz_bits[0]]
        second = [gy_bits[0], gz_bits[1], gz_bits[0], gy_bits[1]]
        rest = gy_bits[2:] + gz_bits[2:]
    return lambda index: (first if index % ny % 2 == 0 else second) + rest


def tree_allreduce(packed, nz, ny, windows, first_step):
    orders = tree_dims(nz, ny)
    count = nz * ny
    steps = len(orders(0))
    lane_steps = min(steps, 3)

    def bit(index, dim):
        row, col = divmod(index, ny)
        return ((row if dim[0] == "gz" else col) >> dim[1]) & 1

    def partner(index, dim):
        row, col = divmod(index, ny)
        if dim[0] == "gz":
            row ^= 1 << dim[1]
        else:
            col ^= 1 << dim[1]
        return row * ny + col

    me = lax.axis_index("gz") * ny + lax.axis_index("gy")
    table = jnp.array([[bit(i, orders(i)[k]) for k in range(steps)] for i in range(count)], jnp.int32)
    mine = table[me]
    pairs = [[(i, partner(i, orders(i)[k])) for i in range(count)] for k in range(steps)]
    results = {}

    def exchange(send, k, key):
        if key not in windows:
            return lax.ppermute(send, ("gz", "gy"), pairs[k])
        work, inputs = windows[key]
        if callable(inputs):
            inputs = inputs(results)
        send, inputs = lax.optimization_barrier((send, inputs))
        got = lax.ppermute(send, ("gz", "gy"), pairs[k])
        outputs = work(*inputs)
        got, results[key] = lax.optimization_barrier((got, outputs))
        return got

    halving = max(steps - 1, 1)
    for k in range(halving):
        axis = 1 if k < lane_steps else 0
        if k == 0:
            keep, send = first_step(mine[0])
        else:
            half = packed.shape[axis] // 2
            keep = lax.dynamic_slice_in_dim(packed, mine[k] * half, half, axis)
            send = lax.dynamic_slice_in_dim(packed, (1 - mine[k]) * half, half, axis)
        packed = keep + exchange(send, k, k)
    for k in range(halving, steps):
        packed = packed + exchange(packed, k, k)
    for k in reversed(range(1, halving)):
        axis = 1 if k < lane_steps else 0
        got = exchange(packed, k, steps + k)
        low = mine[k] == 0
        packed = jnp.concatenate(
            [jnp.where(low, packed, got), jnp.where(low, got, packed)], axis
        )
    got = exchange(packed, 0, steps)
    low = mine[0] == 0
    return (jnp.where(low, packed, got), jnp.where(low, got, packed)), results


def roll_diff(field):
    return (jnp.roll(field, -1, 3) - jnp.roll(field, 1, 3)) * 0.5


def shards(velocity, slip, rate, owner, cell, count, w_in, b_in, w_mid, b_mid, w_out, tau_bar):
    nparts = slip.shape[1]
    slabs = lax.axis_size("gz")
    capacity = 2 * nparts // slabs
    width_all = slabs * capacity
    ncz, ncy, ncx = (velocity.shape[1], velocity.shape[2], velocity.shape[3])
    ncells = ncz * ncy * ncx
    padded = with_halo(velocity, (("gz", 1), ("gy", 2)), 1)
    core = padded[:, 1:-1, 1:-1]
    along_z = (padded[:, 2:, 1:-1] - padded[:, :-2, 1:-1]) * 0.5
    along_y = (padded[:, 1:-1, 2:] - padded[:, 1:-1, :-2]) * 0.5
    grads = jnp.stack([along_z, along_y, roll_diff(core)], 1).reshape(9, ncells)
    live = jnp.arange(nparts, dtype=jnp.int32) < count[0]
    force = jnp.where(live[None, :], rate[None, :] * slip, 0.0)
    owners = owner[:, 0]
    member = (owners[:, None] == jnp.arange(slabs, dtype=jnp.int32)[None, :]).astype(jnp.int32)
    before = jnp.cumsum(member, 0) - member
    position = jnp.sum(before * member, 1)
    slot = owners * capacity + position
    payload = jnp.concatenate(
        [force, jnp.where(live, cell, -1).astype(jnp.float32)[None]], 0
    )
    base = jnp.concatenate(
        [jnp.zeros((3, width_all), jnp.float32), jnp.full((1, width_all), -1.0, jnp.float32)], 0
    )
    received = lax.all_to_all(
        base.at[:, slot].set(payload), "gz", split_axis=1, concat_axis=1, tiled=True
    )
    recv_force = received[:3]
    recv_cell = received[3:].astype(jnp.int32)
    source = deposit(recv_force, recv_cell, ncells)
    feats = jnp.concatenate([grads, source], 0).astype(jnp.bfloat16)
    tbar = tau_bar.reshape(tau_bar.shape[0], ncells)
    pre1 = jnp.einsum("fh,fc->hc", w_in, feats, preferred_element_type=jnp.float32) + b_in[:, None]
    hidden_one = jax.nn.silu(pre1).astype(jnp.bfloat16)
    pre2 = (
        jnp.einsum("gh,gc->hc", w_mid, hidden_one, preferred_element_type=jnp.float32)
        + b_mid[:, None]
    )
    hidden_two = jax.nn.silu(pre2).astype(jnp.bfloat16)
    stress = jnp.einsum("ho,hc->oc", w_out, hidden_two, preferred_element_type=jnp.float32)
    grad_w_out_t = jnp.einsum("oc,hc->oh", tbar, hidden_two, preferred_element_type=jnp.float32)
    back_two = jnp.einsum("ho,oc->hc", w_out, tbar, preferred_element_type=jnp.float32)
    delta_two = (back_two * dsilu(pre2)).astype(jnp.bfloat16)
    back_one = jnp.einsum("gh,hc->gc", w_mid, delta_two, preferred_element_type=jnp.float32)
    delta_one = (back_one * dsilu(pre1)).astype(jnp.bfloat16)
    grad_w_in = jnp.einsum("fc,hc->fh", feats, delta_one, preferred_element_type=jnp.float32)
    grad_b_in = jnp.sum(delta_one.astype(jnp.float32), 1)
    nz, ny = lax.axis_size("gz"), lax.axis_size("gy")
    count = nz * ny
    feats_bar = jnp.einsum("fh,hc->fc", w_in, delta_one, preferred_element_type=jnp.float32)

    def z_work(feats_bar):
        grads_bar = feats_bar[:9].reshape(3, 3, ncz, ncy, ncx)
        zpad = with_halo(grads_bar[:, 0], (("gz", 1),), 1)
        return (zpad[:, 2:] - zpad[:, :-2]) * 0.5

    def y_work(feats_bar):
        grads_bar = feats_bar[:9].reshape(3, 3, ncz, ncy, ncx)
        ypad = with_halo(grads_bar[:, 1], (("gy", 2),), 1)
        return (ypad[:, :, 2:] - ypad[:, :, :-2]) * 0.5

    def collect_work(feats_bar, recv_cell):
        return collect(feats_bar[9:12], recv_cell, ncells)

    def particle_work(per_slot, slot, live, rate, slip):
        returned = lax.all_to_all(per_slot, "gz", split_axis=1, concat_axis=1, tiled=True)
        at_particle = returned[:, slot]
        slip_bar = jnp.where(live[None, :], rate[None, :] * at_particle, 0.0)
        rate_bar = jnp.where(live, jnp.sum(slip * at_particle, 0), 0.0)
        return slip_bar, rate_bar

    steps = (count - 1).bit_length()
    row_steps = max(steps - 3, 0)
    nh = hidden_one.shape[0]
    grad_b_mid = jnp.sum(delta_two.astype(jnp.float32), 1)
    small = jnp.concatenate([grad_b_mid[None], grad_w_in, grad_b_in[None], grad_w_out_t], 0)
    rows_needed = nh + small.shape[0]
    unit = 8 << row_steps
    rows_total = -(-rows_needed // unit) * unit
    left = jnp.pad(hidden_one, ((0, rows_total - nh), (0, 0)))
    half = delta_two.shape[0] // 2

    def first_step(low_bit):
        def part(offset):
            right = lax.dynamic_slice_in_dim(delta_two, offset, half, 0)
            out = jnp.einsum("gc,hc->gh", left, right, preferred_element_type=jnp.float32)
            extra = lax.dynamic_slice_in_dim(small, offset, half, 1)
            return out + jnp.pad(extra, ((nh, rows_total - rows_needed), (0, 0)))

        return part(low_bit * half), part((1 - low_bit) * half)

    windows = {
        1: (z_work, (feats_bar,)),
        2: (y_work, (feats_bar,)),
        3: (collect_work, (feats_bar, recv_cell)),
        steps + 1: (particle_work, lambda done: (done[3], slot, live, rate, slip)),
    }
    (low_part, high_part), results = tree_allreduce(None, nz, ny, windows, first_step)
    packed = jnp.concatenate([low_part, high_part], 1)
    slip_bar, rate_bar = results[steps + 1]
    term_x = roll_diff(feats_bar[:9].reshape(3, 3, ncz, ncy, ncx)[:, 2])
    velocity_bar = -(results[1] + results[2] + term_x)
    grad_w_mid = packed[:nh]
    grad_b_mid = packed[nh]
    grad_w_in = packed[nh + 1 : nh + 1 + grad_w_in.shape[0]]
    start = nh + 1 + grad_w_in.shape[0]
    grad_b_in = packed[start]
    grad_w_out = packed[start + 1 : start + 1 + grad_w_out_t.shape[0]].T
    return (
        stress.reshape(stress.shape[0], ncz, ncy, ncx),
        velocity_bar,
        slip_bar,
        rate_bar,
        grad_w_in,
        grad_b_in,
        grad_w_mid,
        grad_b_mid,
        grad_w_out,
    )


def solution(mesh):
    return jax.shard_map(
        shards,
        mesh=mesh,
        in_specs=(
            P(None, "gz", "gy", None),
            P(None, ("gz", "gy")),
            P(("gz", "gy")),
            P(("gz", "gy"), None),
            P(("gz", "gy")),
            P(("gz", "gy")),
            P(),
            P(),
            P(),
            P(),
            P(),
            P(None, "gz", "gy", None),
        ),
        out_specs=(
            P(None, "gz", "gy", None),
            P(None, "gz", "gy", None),
            P(None, ("gz", "gy")),
            P(("gz", "gy")),
            P(),
            P(),
            P(),
            P(),
            P(),
        ),
        check_vma=False,
    )
```
